128 devices in a mesh: tok: 8 (over z, y_hi), head: 16 (over x, y_lo, core).
Axes of the slice: x: 4, y: 4 (y_hi: 2, y_lo: 2; y = y_hi * 2 + y_lo), z: 4, core: 2. Of those that a mesh axis runs over, the one named last changes fastest.
Arguments:
- states: bfloat16 [4096, 4096], P('tok', 'head'), may hold values from -400 to 400
- pre_gain: float32 [4096], replicated, may hold values from 0.5 to 1.5
- pre_shift: float32 [4096], replicated, may hold values from -1.75 to 1.75
- mlp_gain: float32 [4096], replicated, may hold values from 0.5 to 1.5
- mlp_shift: float32 [4096], replicated, may hold values from -1.75 to 1.75
- qkv_weight: bfloat16 [4096, 12288], P('tok', 'head'), may hold values from -0.09375 to 0.09375
- qkv_bias: float32 [12288], P('head'), may hold values from -1.75 to 1.75
- out_weight: bfloat16 [4096, 4096], P('head', 'tok'), may hold values from -0.125 to 0.125
- out_bias: float32 [4096], P('head'), may hold values from -1.75 to 1.75
- up_weight: bfloat16 [4096, 16384], P(None, 'head'), may hold values from -0.09375 to 0.09375
- up_bias: float32 [16384], P('head'), may hold values from -1.75 to 1.75
- down_weight: bfloat16 [16384, 4096], P('head'), may hold values from -0.0625 to 0.0625
- down_bias: float32 [4096], P('head'), may hold values from -1.75 to 1.75
- kv_cache: bfloat16 [1152, 2, 16, 4096], P(('tok', 'head')), may hold values from -320 to 320, as said below
- token_request: int32 [4096], P('tok'), may hold values from 0 to 15, as said below
- cached_len: int32 [16], P('tok'), may hold values from 128 to 1024, as said below
- page_table: int32 [16, 64], P('tok'), may hold values from 0 to 143, as said below
- migrations: int32 [64, 2], P('tok'), may hold values from 0 to 143, as said below
Outputs:
- update: bfloat16 [4096, 4096], P('tok', 'head')
The draws below stay inside these ranges and needn't reach their ends.
Inputs may be any that keep to these rules, and one draw needn't show every extreme that they name: `token_request`: ids never fall; the tokens of request r lie among tokens (r // 2) * 512 to that plus 512 - 1, and every request has one token or more. `cached_len`: some request holds exactly 1024. `page_table`: the entries of one block are distinct. `migrations`: targets of one block are distinct and none is also a source of that block. `kv_cache`: keys are stored already rotated.
All inputs are finite; a program needn't handle non-finite values.
Results may differ from the reference program's by a relative error of at most 0.018.
The reference program's roundings to bfloat16 on the way count: a program that leaves them out, or rounds other values in their place, can miss the bound.
Values may be sent and summed in bfloat16 or wider, within the bound.
No kernel may reach another device: no remote copies, remote signals or barrier semaphores. Data moves between devices by JAX's collectives and lax.ppermute only.
A program may use at most 128 MiB of HBM per device.

```python
from functools import partial
import jax
import jax.numpy as jnp
from jax import lax

D = 4096
HEADS = 32
HD = 128
FF = 16384
ROT = 32
TOK_DEV = 512
REQ_TOK = 2
CACHE_MAX = 1024
PAGE = 16
MIG_REQ = 4
TOKENS = 4096
REQS = 16
MAX_PAGES = 64
MIG = 8
SLOTS = 144


def draw_states(key, part):
    subkeys = jax.random.split(key, 3)
    row_scale = 10.0 ** jax.random.uniform(subkeys[0], (TOKENS, 1), jnp.float32)
    col_scale = 10.0 ** jax.random.uniform(subkeys[1], (1, D), jnp.float32)
    normal_draw = jnp.clip(jax.random.normal(subkeys[2], (TOKENS, D), jnp.float32), -4.0, 4.0)
    return (normal_draw * row_scale * col_scale).astype(jnp.bfloat16)


def draw_kv_cache(key, part):
    slot_count = REQS // REQ_TOK * SLOTS
    shape_full = (slot_count, 2, PAGE, HEADS * HD)
    key_scale = jnp.array([1.5, 1.0], jnp.float32)[None, :, None, None]
    base_key = jax.random.fold_in(key, 20)
    normal_draw = jnp.clip(jax.random.normal(base_key, shape_full, jnp.float32), -6.0, 6.0)
    return (normal_draw * key_scale).astype(jnp.bfloat16)


def block_requests(key, block_index):
    block_key = jax.random.fold_in(jax.random.fold_in(key, 13), block_index)
    cut_points = jax.random.permutation(block_key, TOK_DEV - 1)[:REQ_TOK - 1].astype(jnp.int32) + 1
    places = jnp.arange(TOK_DEV, dtype=jnp.int32)
    inside = jnp.sum((places[:, None] >= cut_points[None, :]).astype(jnp.int32), axis=1)
    return (block_index * REQ_TOK + inside).astype(jnp.int32)


def draw_token_request(key, part):
    blocks = REQS // REQ_TOK
    return jax.vmap(partial(block_requests, key))(jnp.arange(blocks, dtype=jnp.int32)).reshape(TOKENS)


def draw_cached_len(key, part):
    lengths = jax.random.randint(jax.random.fold_in(key, 11), (REQS,), CACHE_MAX // 8, CACHE_MAX + 1).astype(jnp.int32)
    longest = jax.random.randint(jax.random.fold_in(key, 12), (), 0, REQS)
    return lengths.at[longest].set(CACHE_MAX)


def page_layout(key, block_index):
    block_key = jax.random.fold_in(jax.random.fold_in(key, 7), block_index)
    shuffled = jax.random.permutation(block_key, SLOTS).astype(jnp.int32)
    in_use = shuffled[:REQ_TOK * MAX_PAGES].reshape(REQ_TOK, MAX_PAGES)
    spare_slots = shuffled[REQ_TOK * MAX_PAGES:REQ_TOK * MAX_PAGES + MIG]
    early_pages = CACHE_MAX // (8 * PAGE)

    def chosen(request):
        picked_pages = jax.random.permutation(jax.random.fold_in(block_key, 1000 + request), early_pages)[:MIG_REQ]
        return in_use[request, picked_pages]
    targets = jax.vmap(chosen)(jnp.arange(REQ_TOK, dtype=jnp.int32)).reshape(MIG)
    return (in_use, jnp.stack([spare_slots, targets], axis=1).astype(jnp.int32))


def draw_page_table(key, part):
    blocks = REQS // REQ_TOK
    tables, moves = jax.vmap(partial(page_layout, key))(jnp.arange(blocks, dtype=jnp.int32))
    return tables.reshape(REQS, MAX_PAGES)


def draw_migrations(key, part):
    blocks = REQS // REQ_TOK
    tables, moves = jax.vmap(partial(page_layout, key))(jnp.arange(blocks, dtype=jnp.int32))
    return moves.reshape(blocks * MIG, 2)


def strengthened(entries, key, source, target, shards_of, factor):
    owner, partner = [(jnp.arange(entries.shape[axis_at]) // (entries.shape[axis_at] // shards_of)).reshape([-1 if axis == axis_at else 1 for axis in range(entries.ndim)]) for axis_at in (source, target)]
    chosen = jax.random.permutation(key, shards_of)[partner]
    strong = (owner == chosen) | (owner == (partner + shards_of // 2) % shards_of)
    return jnp.where(strong, factor * entries, entries)


def levels(own_key, dims, cuts, low, high):
    def one(axis_at, shards_of):
        heights = jax.random.uniform(jax.random.fold_in(jax.random.fold_in(own_key, 6), axis_at), (shards_of,), jnp.float32, low / len(cuts), high / len(cuts))
        return jnp.repeat(jnp.exp(heights), dims[axis_at] // shards_of).reshape((-1,) + (1,) * (len(dims) - axis_at - 1))

    loudness = one(*cuts[0])
    for cut in cuts[1:]:
        loudness = loudness * one(*cut)
    return loudness


def normal_values(own_key, shape, width, reach, pieces=(), kind=jnp.bfloat16):
    result = width * jax.random.normal(own_key, shape, jnp.float32)
    if pieces:
        result = result * levels(own_key, shape, pieces, -0.22, 0.18)
    return jnp.clip(result, -reach, reach).astype(kind)


def heavy_noise(own_key, dims, spread, reach, shards, heavy, kind=jnp.bfloat16):
    values = spread * jax.random.normal(own_key, dims, jnp.float32)
    if shards:
        values = values * levels(own_key, dims, shards, -0.22, 0.18)
    return jnp.clip(strengthened(values, jax.random.fold_in(own_key, 3), *heavy), -reach, reach).astype(kind)


def setup_inputs(seed: int = 0) -> dict:
    splits = jax.random.split(jax.random.key(seed), 19)
    states = draw_states(jax.random.fold_in(splits[18], 71), 0)
    pre_gain = jnp.clip(1.0 + 0.1 * jax.random.normal(splits[1], (D,), jnp.float32), 0.5, 1.5)
    pre_shift = normal_values(splits[2], (D,), 0.3, 1.75, (), jnp.float32)
    mlp_gain = jnp.clip(1.0 + 0.1 * jax.random.normal(splits[3], (D,), jnp.float32), 0.5, 1.5)
    mlp_shift = normal_values(splits[4], (D,), 0.3, 1.75, (), jnp.float32)
    qkv_weight = normal_values(splits[5], (D, 3 * HEADS * HD), D ** -0.5, 0.09375, ((0, 8), (1, 16)))
    qkv_bias = normal_values(splits[6], (3 * HEADS * HD,), 0.3, 1.75, ((0, 16),), jnp.float32)
    out_weight = heavy_noise(splits[7], (HEADS * HD, D), (HEADS * HD) ** -0.5, 0.125, ((0, 16), (1, 8)), (0, 1, 16, 2.0))
    out_bias = normal_values(splits[8], (D,), 0.3, 1.75, ((0, 16),), jnp.float32)
    up_weight = normal_values(splits[9], (D, FF), D ** -0.5, 0.09375, ((1, 16),))
    up_bias = normal_values(splits[10], (FF,), 0.3, 1.75, ((0, 16),), jnp.float32)
    down_weight = heavy_noise(splits[11], (FF, D), FF ** -0.5, 0.0625, ((0, 16),), (0, 1, 16, 2.0))
    down_bias = normal_values(splits[12], (D,), 0.3, 1.75, ((0, 16),), jnp.float32)
    kv_cache = draw_kv_cache(jax.random.fold_in(splits[18], 71), 0)
    token_request = draw_token_request(jax.random.fold_in(splits[18], 71), 0)
    cached_len = draw_cached_len(jax.random.fold_in(splits[18], 71), 0)
    page_table = draw_page_table(jax.random.fold_in(splits[18], 71), 0)
    migrations = draw_migrations(jax.random.fold_in(splits[18], 71), 0)
    return {"states": states, "pre_gain": pre_gain, "pre_shift": pre_shift, "mlp_gain": mlp_gain, "mlp_shift": mlp_shift, "qkv_weight": qkv_weight, "qkv_bias": qkv_bias, "out_weight": out_weight, "out_bias": out_bias, "up_weight": up_weight, "up_bias": up_bias, "down_weight": down_weight, "down_bias": down_bias, "kv_cache": kv_cache, "token_request": token_request, "cached_len": cached_len, "page_table": page_table, "migrations": migrations}


epsilon = 1e-05

def layer_norm(wide, gain, shift):
    row_mean = lax.optimization_barrier(jnp.mean(wide, axis=1, keepdims=True))
    centred = wide - row_mean
    row_var = lax.optimization_barrier(jnp.mean(centred * centred, axis=1, keepdims=True))
    return (centred * lax.rsqrt(row_var + epsilon) * gain + shift).astype(jnp.bfloat16)

def rotate(vectors, positions):
    half_rot = ROT // 2
    inv_freq = 10000.0 ** (-2.0 * jnp.arange(half_rot, dtype=jnp.float32) / ROT)
    angles = positions.astype(jnp.float32)[:, None] * inv_freq[None, :]
    cosine = jnp.cos(angles)[:, None, :]
    sine_part = jnp.sin(angles)[:, None, :]
    lower_half = vectors[..., :half_rot]
    upper_half = vectors[..., half_rot:ROT]
    return jnp.concatenate([lower_half * cosine - upper_half * sine_part, upper_half * cosine + lower_half * sine_part, vectors[..., ROT:]], axis=-1)

def token_positions(local_req, cached):
    onehot = local_req[:, None] == jnp.arange(cached.shape[0], dtype=jnp.int32)[None, :]
    stretch_sizes = lax.optimization_barrier(jnp.sum(onehot.astype(jnp.int32), axis=0))
    starts = jnp.cumsum(stretch_sizes) - stretch_sizes
    own_start = lax.optimization_barrier(jnp.sum(jnp.where(onehot, starts[None, :], 0), axis=1))
    own_cached = lax.optimization_barrier(jnp.sum(jnp.where(onehot, cached[None, :], 0), axis=1))
    return own_cached + jnp.arange(local_req.shape[0], dtype=jnp.int32) - own_start

def attend(queries, new_keys, new_values, cache_keys, cache_values, local_req, cached, positions):
    span = cache_keys.shape[0] // cached.shape[0]
    key_slot = jnp.arange(cache_keys.shape[0], dtype=jnp.int32)
    key_owner = key_slot // span
    key_place = key_slot % span
    cache_ok = (local_req[:, None] == key_owner[None, :]) & (key_place[None, :] < jnp.repeat(cached, span)[None, :])
    new_ok = (local_req[:, None] == local_req[None, :]) & (positions[None, :] <= positions[:, None])
    allowed = jnp.concatenate([cache_ok, new_ok], axis=1)
    all_keys = jnp.concatenate([cache_keys, new_keys], axis=0).astype(jnp.float32)
    all_values = jnp.concatenate([cache_values, new_values], axis=0).astype(jnp.float32)
    scores = jnp.einsum('thd,khd->htk', queries.astype(jnp.float32), all_keys) * HD ** (-0.5)
    scores = jnp.where(allowed[None], scores, -1e+30)
    peak = lax.optimization_barrier(jnp.max(scores, axis=2, keepdims=True))
    exp_scores = jnp.exp(scores - peak)
    attn_probs = (exp_scores / lax.optimization_barrier(jnp.sum(exp_scores, axis=2, keepdims=True))).astype(jnp.bfloat16)
    return jnp.einsum('htk,khd->thd', attn_probs.astype(jnp.float32), all_values).astype(jnp.bfloat16)

def reference(states, pre_gain, pre_shift, mlp_gain, mlp_shift, qkv_weight, qkv_bias, out_weight, out_bias, up_weight, up_bias, down_weight, down_bias, kv_cache, token_request, cached_len, page_table, migrations):
    wide = states.astype(jnp.float32)
    pre_normed = layer_norm(wide, pre_gain, pre_shift)
    mlp_normed = layer_norm(wide, mlp_gain, mlp_shift)
    joined = (jnp.dot(pre_normed, qkv_weight, preferred_element_type=jnp.float32) + qkv_bias).reshape(TOKENS, HEADS, 3, HD)
    blocks = TOKENS // TOK_DEV
    block_base = jnp.arange(TOKENS, dtype=jnp.int32) // TOK_DEV * REQ_TOK
    local_req = token_request - block_base
    positions = jax.vmap(token_positions)(local_req.reshape(blocks, TOK_DEV), cached_len.reshape(blocks, REQ_TOK)).reshape(TOKENS)
    queries = rotate(joined[:, :, 0], positions).astype(jnp.bfloat16)
    new_keys = rotate(joined[:, :, 1], positions).astype(jnp.bfloat16)
    new_values = joined[:, :, 2].astype(jnp.bfloat16)
    pools = kv_cache.reshape(blocks, SLOTS, 2, PAGE, HEADS * HD)

    def one_block(inputs):
        block_queries, block_keys, block_values, block_req, block_cached, block_pos, page_pool, block_table, block_moves = inputs
        page_pool = page_pool.at[block_moves[:, 1]].set(page_pool[block_moves[:, 0]])
        pages = page_pool[block_table.reshape(-1)]
        cache_keys = pages[:, 0].reshape(-1, HEADS, HD)
        cache_values = pages[:, 1].reshape(-1, HEADS, HD)
        return attend(block_queries, block_keys, block_values, cache_keys, cache_values, block_req, block_cached, block_pos)
    mixed = lax.map(one_block, (queries.reshape(blocks, TOK_DEV, HEADS, HD), new_keys.reshape(blocks, TOK_DEV, HEADS, HD), new_values.reshape(blocks, TOK_DEV, HEADS, HD), local_req.reshape(blocks, TOK_DEV), cached_len.reshape(blocks, REQ_TOK), positions.reshape(blocks, TOK_DEV), pools, page_table.reshape(blocks, REQ_TOK, MAX_PAGES), migrations.reshape(blocks, MIG, 2)))
    heads_out = mixed.reshape(TOKENS, HEADS * HD)
    attention = jnp.dot(heads_out, out_weight, preferred_element_type=jnp.float32) + out_bias
    hidden = jax.nn.gelu(jnp.dot(mlp_normed, up_weight, preferred_element_type=jnp.float32) + up_bias, approximate=False).astype(jnp.bfloat16)
    feed = jnp.dot(hidden, down_weight, preferred_element_type=jnp.float32) + down_bias
    return (attention + feed).astype(jnp.bfloat16)
```

```python
import jax
import jax.numpy as jnp
from jax import lax
from jax.sharding import PartitionSpec as P

HD = 128
ROT = 32


epsilon = 1e-05


def layer_norm(wide, gain, shift):
    row_mean = jnp.mean(wide, axis=1, keepdims=True)
    centred = wide - row_mean
    row_var = jnp.mean(centred * centred, axis=1, keepdims=True)
    return (centred * lax.rsqrt(row_var + epsilon) * gain + shift).astype(jnp.bfloat16)


def rotate(vectors, positions):
    half_rot = ROT // 2
    inv_freq = 10000.0 ** (-2.0 * jnp.arange(half_rot, dtype=jnp.float32) / ROT)
    angles = positions.astype(jnp.float32)[:, None] * inv_freq[None, :]
    cosine = jnp.cos(angles)[:, None, :]
    sine_part = jnp.sin(angles)[:, None, :]
    lower_half = vectors[..., :half_rot]
    upper_half = vectors[..., half_rot:ROT]
    return jnp.concatenate(
        [
            lower_half * cosine - upper_half * sine_part,
            upper_half * cosine + lower_half * sine_part,
            vectors[..., ROT:],
        ],
        axis=-1,
    )


def token_positions(local_req, cached):
    onehot = local_req[:, None] == jnp.arange(cached.shape[0], dtype=jnp.int32)[None, :]
    stretch_sizes = jnp.sum(onehot.astype(jnp.int32), axis=0)
    starts = jnp.cumsum(stretch_sizes) - stretch_sizes
    own_start = jnp.sum(jnp.where(onehot, starts[None, :], 0), axis=1)
    own_cached = jnp.sum(jnp.where(onehot, cached[None, :], 0), axis=1)
    return own_cached + jnp.arange(local_req.shape[0], dtype=jnp.int32) - own_start


def attend(queries, new_keys, new_values, cache_keys, cache_values, local_req, cached, positions):
    span = cache_keys.shape[0] // cached.shape[0]
    key_slot = jnp.arange(cache_keys.shape[0], dtype=jnp.int32)
    key_owner = key_slot // span
    key_place = key_slot % span
    cache_ok = (local_req[:, None] == key_owner[None, :]) & (
        key_place[None, :] < jnp.repeat(cached, span)[None, :]
    )
    new_ok = (local_req[:, None] == local_req[None, :]) & (positions[None, :] <= positions[:, None])
    allowed = jnp.concatenate([cache_ok, new_ok], axis=1)
    all_keys = jnp.concatenate([cache_keys, new_keys], axis=0)
    all_values = jnp.concatenate([cache_values, new_values], axis=0)
    scores = jnp.einsum(
        "thd,khd->htk", queries, all_keys, preferred_element_type=jnp.float32
    ) * HD ** (-0.5)
    scores = jnp.where(allowed[None], scores, -1e30)
    peak = jnp.max(scores, axis=2, keepdims=True)
    exp_scores = jnp.exp(scores - peak)
    attn_probs = (exp_scores / jnp.sum(exp_scores, axis=2, keepdims=True)).astype(jnp.bfloat16)
    return jnp.einsum(
        "htk,khd->thd", attn_probs, all_values, preferred_element_type=jnp.float32
    ).astype(jnp.bfloat16)


def share_pages(local_pool, groups):
    grouped = local_pool.reshape(
        local_pool.shape[0], 2, local_pool.shape[2], groups, local_pool.shape[3] // groups
    )
    shared = lax.all_to_all(grouped, "head", split_axis=3, concat_axis=0, tiled=True)
    return shared.reshape(shared.shape[0], 2, shared.shape[2], shared.shape[4])


def shards(
    states,
    pre_gain,
    pre_shift,
    mlp_gain,
    mlp_shift,
    qkv_weight,
    qkv_bias,
    out_weight,
    out_bias,
    up_weight,
    up_bias,
    down_weight,
    down_bias,
    kv_cache,
    token_request,
    cached_len,
    page_table,
    migrations,
):
    gathered = lax.all_gather(states, "head", axis=1, tiled=True)
    wide = gathered.astype(jnp.float32)
    pre_normed = layer_norm(wide, pre_gain, pre_shift)
    mlp_normed = layer_norm(wide, mlp_gain, mlp_shift)
    tok_rows = gathered.shape[0]
    joined = jnp.dot(
        pre_normed,
        lax.all_gather(qkv_weight, "tok", axis=0, tiled=True),
        preferred_element_type=jnp.float32,
    )
    joined = (joined + qkv_bias).reshape(tok_rows, -1, 3, HD)
    local_req = token_request - lax.axis_index("tok") * cached_len.shape[0]
    positions = token_positions(local_req, cached_len)
    queries = rotate(joined[:, :, 0], positions).astype(jnp.bfloat16)
    new_keys = rotate(joined[:, :, 1], positions).astype(jnp.bfloat16)
    new_values = joined[:, :, 2].astype(jnp.bfloat16)
    head_groups = lax.axis_size("head")
    sources = migrations[:, 0]
    targets = migrations[:, 1]
    page_pool = share_pages(kv_cache, head_groups)
    table = page_table.reshape(-1)
    match = table[:, None] == targets[None, :]
    moved_from = jnp.sum(jnp.where(match, sources[None, :], 0), axis=1)
    table = jnp.where(jnp.any(match, axis=1), moved_from, table)
    pages = page_pool[table]
    cache_keys = pages[:, 0].reshape(-1, queries.shape[1], HD)
    cache_values = pages[:, 1].reshape(-1, queries.shape[1], HD)
    heads_out = attend(
        queries, new_keys, new_values, cache_keys, cache_values, local_req, cached_len, positions
    ).reshape(tok_rows, -1)
    attention_part = jnp.dot(
        heads_out,
        lax.all_gather(out_weight, "tok", axis=1, tiled=True),
        preferred_element_type=jnp.float32,
    )
    hidden = jax.nn.gelu(
        jnp.dot(mlp_normed, up_weight, preferred_element_type=jnp.float32) + up_bias,
        approximate=False,
    ).astype(jnp.bfloat16)
    feed_part = jnp.dot(hidden, down_weight, preferred_element_type=jnp.float32)
    summed = lax.psum_scatter(
        (attention_part + feed_part).astype(jnp.bfloat16), "head", scatter_dimension=1, tiled=True
    ).astype(jnp.float32)
    return (summed + out_bias + down_bias).astype(jnp.bfloat16)


def solution(mesh):
    in_specs = (
        P("tok", "head"),
        P(),
        P(),
        P(),
        P(),
        P("tok", "head"),
        P("head"),
        P("head", "tok"),
        P("head"),
        P(None, "head"),
        P("head"),
        P("head", None),
        P("head"),
        P(("tok", "head"), None, None, None),
        P("tok"),
        P("tok"),
        P("tok", None),
        P("tok", None),
    )
    out_specs = P("tok", "head")
    return jax.shard_map(shards, mesh=mesh, in_specs=in_specs, out_specs=out_specs, check_vma=False)
```

```python
import jax
import jax.numpy as jnp
from jax import lax
from jax.sharding import PartitionSpec as P

HD = 128
ROT = 32


epsilon = 1e-05


def layer_norm(wide, gain, shift):
    row_mean = jnp.mean(wide, axis=1, keepdims=True)
    centred = wide - row_mean
    row_var = jnp.mean(centred * centred, axis=1, keepdims=True)
    return (centred * lax.rsqrt(row_var + epsilon) * gain + shift).astype(jnp.bfloat16)


def rotate(vectors, positions):
    half_rot = ROT // 2
    inv_freq = 10000.0 ** (-2.0 * jnp.arange(half_rot, dtype=jnp.float32) / ROT)
    angles = positions.astype(jnp.float32)[:, None] * inv_freq[None, :]
    cosine = jnp.cos(angles)[:, None, :]
    sine_part = jnp.sin(angles)[:, None, :]
    lower_half = vectors[..., :half_rot]
    upper_half = vectors[..., half_rot:ROT]
    return jnp.concatenate(
        [
            lower_half * cosine - upper_half * sine_part,
            upper_half * cosine + lower_half * sine_part,
            vectors[..., ROT:],
        ],
        axis=-1,
    )


def token_positions(local_req, cached):
    onehot = local_req[:, None] == jnp.arange(cached.shape[0], dtype=jnp.int32)[None, :]
    stretch_sizes = jnp.sum(onehot.astype(jnp.int32), axis=0)
    starts = jnp.cumsum(stretch_sizes) - stretch_sizes
    own_start = jnp.sum(jnp.where(onehot, starts[None, :], 0), axis=1)
    own_cached = jnp.sum(jnp.where(onehot, cached[None, :], 0), axis=1)
    return own_cached + jnp.arange(local_req.shape[0], dtype=jnp.int32) - own_start


def attend(queries, new_keys, new_values, cache_keys, cache_values, local_req, cached, positions):
    span = cache_keys.shape[0] // cached.shape[0]
    key_slot = jnp.arange(cache_keys.shape[0], dtype=jnp.int32)
    key_owner = key_slot // span
    key_place = key_slot % span
    cache_ok = (local_req[:, None] == key_owner[None, :]) & (
        key_place[None, :] < jnp.repeat(cached, span)[None, :]
    )
    new_ok = (local_req[:, None] == local_req[None, :]) & (positions[None, :] <= positions[:, None])
    allowed = jnp.concatenate([cache_ok, new_ok], axis=1)
    all_keys = jnp.concatenate([cache_keys, new_keys], axis=0)
    all_values = jnp.concatenate([cache_values, new_values], axis=0)
    scores = jnp.einsum(
        "thd,khd->htk", queries, all_keys, preferred_element_type=jnp.float32
    ) * HD ** (-0.5)
    scores = jnp.where(allowed[None], scores, -1e30)
    peak = jnp.max(scores, axis=2, keepdims=True)
    exp_scores = jnp.exp(scores - peak)
    attn_probs = (exp_scores / jnp.sum(exp_scores, axis=2, keepdims=True)).astype(jnp.bfloat16)
    return jnp.einsum(
        "htk,khd->thd", attn_probs, all_values, preferred_element_type=jnp.float32
    ).astype(jnp.bfloat16)


def share_pages(local_pool, groups):
    grouped = local_pool.reshape(
        local_pool.shape[0], 2, local_pool.shape[2], groups, local_pool.shape[3] // groups
    )
    shared = lax.all_to_all(grouped, "head", split_axis=3, concat_axis=0, tiled=True)
    return shared.reshape(shared.shape[0], 2, shared.shape[2], shared.shape[4])


def tok_blocks(block):
    count = lax.axis_size("tok")
    me = lax.axis_index("tok")
    received = [(me, block)]
    for shift in range(1, count):
        perm = [(i, (i + shift) % count) for i in range(count)]
        received.append(((me - shift) % count, lax.ppermute(block, "tok", perm)))
    return received


def qkv_by_blocks(pre_normed, qkv_weight):
    rows = qkv_weight.shape[0]
    total = None
    for owner, block in tok_blocks(qkv_weight):
        part = lax.dynamic_slice_in_dim(pre_normed, owner * rows, rows, axis=1)
        product = jnp.dot(part, block, preferred_element_type=jnp.float32)
        total = product if total is None else total + product
    return total


def gather_tok_columns(out_weight):
    cols = out_weight.shape[1]
    full = jnp.zeros((out_weight.shape[0], cols * lax.axis_size("tok")), out_weight.dtype)
    for owner, block in tok_blocks(out_weight):
        full = lax.dynamic_update_slice_in_dim(full, block, owner * cols, axis=1)
    return full


def shards(
    states,
    pre_gain,
    pre_shift,
    mlp_gain,
    mlp_shift,
    qkv_weight,
    qkv_bias,
    out_weight,
    out_bias,
    up_weight,
    up_bias,
    down_weight,
    down_bias,
    kv_cache,
    token_request,
    cached_len,
    page_table,
    migrations,
):
    gathered = lax.all_gather(states, "head", axis=1, tiled=True)
    wide = gathered.astype(jnp.float32)
    pre_normed = layer_norm(wide, pre_gain, pre_shift)
    mlp_normed = layer_norm(wide, mlp_gain, mlp_shift)
    tok_rows = gathered.shape[0]
    joined = qkv_by_blocks(pre_normed, qkv_weight)
    joined = (joined + qkv_bias).reshape(tok_rows, -1, 3, HD)
    local_req = token_request - lax.axis_index("tok") * cached_len.shape[0]
    positions = token_positions(local_req, cached_len)
    queries = rotate(joined[:, :, 0], positions).astype(jnp.bfloat16)
    new_keys = rotate(joined[:, :, 1], positions).astype(jnp.bfloat16)
    new_values = joined[:, :, 2].astype(jnp.bfloat16)
    head_groups = lax.axis_size("head")
    sources = migrations[:, 0]
    targets = migrations[:, 1]
    page_pool = share_pages(kv_cache, head_groups)
    table = page_table.reshape(-1)
    match = table[:, None] == targets[None, :]
    moved_from = jnp.sum(jnp.where(match, sources[None, :], 0), axis=1)
    table = jnp.where(jnp.any(match, axis=1), moved_from, table)
    pages = page_pool[table]
    cache_keys = pages[:, 0].reshape(-1, queries.shape[1], HD)
    cache_values = pages[:, 1].reshape(-1, queries.shape[1], HD)
    heads_out = attend(
        queries, new_keys, new_values, cache_keys, cache_values, local_req, cached_len, positions
    ).reshape(tok_rows, -1)
    attention_part = jnp.dot(
        heads_out, gather_tok_columns(out_weight), preferred_element_type=jnp.float32
    )
    hidden = jax.nn.gelu(
        jnp.dot(mlp_normed, up_weight, preferred_element_type=jnp.float32) + up_bias,
        approximate=False,
    ).astype(jnp.bfloat16)
    feed_part = jnp.dot(hidden, down_weight, preferred_element_type=jnp.float32)
    summed = lax.psum_scatter(
        (attention_part + feed_part).astype(jnp.bfloat16), "head", scatter_dimension=1, tiled=True
    ).astype(jnp.float32)
    return (summed + out_bias + down_bias).astype(jnp.bfloat16)


def solution(mesh):
    in_specs = (
        P("tok", "head"),
        P(),
        P(),
        P(),
        P(),
        P("tok", "head"),
        P("head"),
        P("head", "tok"),
        P("head"),
        P(None, "head"),
        P("head"),
        P("head", None),
        P("head"),
        P(("tok", "head"), None, None, None),
        P("tok"),
        P("tok"),
        P("tok", None),
        P("tok", None),
    )
    out_specs = P("tok", "head")
    return jax.shard_map(shards, mesh=mesh, in_specs=in_specs, out_specs=out_specs, check_vma=False)
```

```python
import jax
import jax.numpy as jnp
from jax import lax
from jax.sharding import PartitionSpec as P

HD = 128
ROT = 32


epsilon = 1e-05


def layer_norm(wide, gain, shift):
    row_mean = jnp.mean(wide, axis=1, keepdims=True)
    centred = wide - row_mean
    row_var = jnp.mean(centred * centred, axis=1, keepdims=True)
    return (centred * lax.rsqrt(row_var + epsilon) * gain + shift).astype(jnp.bfloat16)


def rotate(vectors, positions):
    half_rot = ROT // 2
    inv_freq = 10000.0 ** (-2.0 * jnp.arange(half_rot, dtype=jnp.float32) / ROT)
    angles = positions.astype(jnp.float32)[:, None] * inv_freq[None, :]
    cosine = jnp.cos(angles)[:, None, :]
    sine_part = jnp.sin(angles)[:, None, :]
    lower_half = vectors[..., :half_rot]
    upper_half = vectors[..., half_rot:ROT]
    return jnp.concatenate(
        [
            lower_half * cosine - upper_half * sine_part,
            upper_half * cosine + lower_half * sine_part,
            vectors[..., ROT:],
        ],
        axis=-1,
    )


def token_positions(local_req, cached):
    onehot = local_req[:, None] == jnp.arange(cached.shape[0], dtype=jnp.int32)[None, :]
    stretch_sizes = jnp.sum(onehot.astype(jnp.int32), axis=0)
    starts = jnp.cumsum(stretch_sizes) - stretch_sizes
    own_start = jnp.sum(jnp.where(onehot, starts[None, :], 0), axis=1)
    own_cached = jnp.sum(jnp.where(onehot, cached[None, :], 0), axis=1)
    return own_cached + jnp.arange(local_req.shape[0], dtype=jnp.int32) - own_start


def attend(queries, new_keys, new_values, cache_keys, cache_values, local_req, cached, positions):
    span = cache_keys.shape[0] // cached.shape[0]
    key_slot = jnp.arange(cache_keys.shape[0], dtype=jnp.int32)
    key_owner = key_slot // span
    key_place = key_slot % span
    cache_ok = (local_req[:, None] == key_owner[None, :]) & (
        key_place[None, :] < jnp.repeat(cached, span)[None, :]
    )
    new_ok = (local_req[:, None] == local_req[None, :]) & (positions[None, :] <= positions[:, None])
    allowed = jnp.concatenate([cache_ok, new_ok], axis=1)
    all_keys = jnp.concatenate([cache_keys, new_keys], axis=0)
    all_values = jnp.concatenate([cache_values, new_values], axis=0)
    scores = jnp.einsum(
        "thd,khd->htk", queries, all_keys, preferred_element_type=jnp.float32
    ) * HD ** (-0.5)
    scores = jnp.where(allowed[None], scores, -1e30)
    peak = jnp.max(scores, axis=2, keepdims=True)
    exp_scores = jnp.exp(scores - peak)
    attn_probs = (exp_scores / jnp.sum(exp_scores, axis=2, keepdims=True)).astype(jnp.bfloat16)
    return jnp.einsum(
        "htk,khd->thd", attn_probs, all_values, preferred_element_type=jnp.float32
    ).astype(jnp.bfloat16)


def share_pages(local_pool, groups):
    grouped = local_pool.reshape(
        local_pool.shape[0], 2, local_pool.shape[2], groups, local_pool.shape[3] // groups
    )
    shared = lax.all_to_all(grouped, "head", split_axis=3, concat_axis=0, tiled=True)
    return shared.reshape(shared.shape[0], 2, shared.shape[2], shared.shape[4])


def gather_by_all_to_all(block, axis):
    copies = jnp.concatenate([block] * lax.axis_size(axis), axis=0)
    return lax.all_to_all(copies, axis, split_axis=0, concat_axis=0, tiled=True)


def shards(
    states,
    pre_gain,
    pre_shift,
    mlp_gain,
    mlp_shift,
    qkv_weight,
    qkv_bias,
    out_weight,
    out_bias,
    up_weight,
    up_bias,
    down_weight,
    down_bias,
    kv_cache,
    token_request,
    cached_len,
    page_table,
    migrations,
):
    gathered = lax.all_gather(states, "head", axis=1, tiled=True)
    qkv_full = gather_by_all_to_all(qkv_weight, "tok")
    out_full = lax.all_gather(out_weight, "tok", axis=1, tiled=True)
    wide = gathered.astype(jnp.float32)
    pre_normed = layer_norm(wide, pre_gain, pre_shift)
    mlp_normed = layer_norm(wide, mlp_gain, mlp_shift)
    tok_rows = gathered.shape[0]
    half = tok_rows // 2

    def feed(normed):
        hidden = jax.nn.gelu(
            jnp.dot(normed, up_weight, preferred_element_type=jnp.float32) + up_bias,
            approximate=False,
        ).astype(jnp.bfloat16)
        return jnp.dot(hidden, down_weight, preferred_element_type=jnp.float32)

    feed_first = feed(mlp_normed[:half])
    kv_cache, feed_first = lax.optimization_barrier((kv_cache, feed_first))
    page_pool = share_pages(kv_cache, lax.axis_size("head"))
    joined = jnp.dot(pre_normed, qkv_full, preferred_element_type=jnp.float32)
    joined = (joined + qkv_bias).reshape(tok_rows, -1, 3, HD)
    local_req = token_request - lax.axis_index("tok") * cached_len.shape[0]
    positions = token_positions(local_req, cached_len)
    queries = rotate(joined[:, :, 0], positions).astype(jnp.bfloat16)
    new_keys = rotate(joined[:, :, 1], positions).astype(jnp.bfloat16)
    new_values = joined[:, :, 2].astype(jnp.bfloat16)
    sources = migrations[:, 0]
    targets = migrations[:, 1]
    table = page_table.reshape(-1)
    match = table[:, None] == targets[None, :]
    moved_from = jnp.sum(jnp.where(match, sources[None, :], 0), axis=1)
    table = jnp.where(jnp.any(match, axis=1), moved_from, table)
    pages = page_pool[table]
    cache_keys = pages[:, 0].reshape(-1, queries.shape[1], HD)
    cache_values = pages[:, 1].reshape(-1, queries.shape[1], HD)
    heads_out = attend(
        queries, new_keys, new_values, cache_keys, cache_values, local_req, cached_len, positions
    ).reshape(tok_rows, -1)
    attention_part = jnp.dot(heads_out, out_full, preferred_element_type=jnp.float32)
    both_first = (attention_part[:half] + feed_first).astype(jnp.bfloat16)
    both_first, normed_second = lax.optimization_barrier((both_first, mlp_normed[half:]))
    summed_first = lax.psum_scatter(both_first, "head", scatter_dimension=1, tiled=True)
    both_second = (attention_part[half:] + feed(normed_second)).astype(jnp.bfloat16)
    summed_second = lax.psum_scatter(both_second, "head", scatter_dimension=1, tiled=True)
    summed = jnp.concatenate([summed_first, summed_second], axis=0).astype(jnp.float32)
    return (summed + out_bias + down_bias).astype(jnp.bfloat16)


def solution(mesh):
    in_specs = (
        P("tok", "head"),
        P(),
        P(),
        P(),
        P(),
        P("tok", "head"),
        P("head"),
        P("head", "tok"),
        P("head"),
        P(None, "head"),
        P("head"),
        P("head", None),
        P("head"),
        P(("tok", "head"), None, None, None),
        P("tok"),
        P("tok"),
        P("tok", None),
        P("tok", None),
    )
    out_specs = P("tok", "head")
    return jax.shard_map(shards, mesh=mesh, in_specs=in_specs, out_specs=out_specs, check_vma=False)
```

```python
import jax
import jax.numpy as jnp
from jax import lax
from jax.sharding import PartitionSpec as P

HD = 128
ROT = 32


epsilon = 1e-05


def layer_norm(wide, gain, shift):
    row_mean = jnp.mean(wide, axis=1, keepdims=True)
    centred = wide - row_mean
    row_var = jnp.mean(centred * centred, axis=1, keepdims=True)
    return (centred * lax.rsqrt(row_var + epsilon) * gain + shift).astype(jnp.bfloat16)


def rotate(vectors, positions):
    half_rot = ROT // 2
    inv_freq = 10000.0 ** (-2.0 * jnp.arange(half_rot, dtype=jnp.float32) / ROT)
    angles = positions.astype(jnp.float32)[:, None] * inv_freq[None, :]
    cosine = jnp.cos(angles)[:, None, :]
    sine_part = jnp.sin(angles)[:, None, :]
    lower_half = vectors[..., :half_rot]
    upper_half = vectors[..., half_rot:ROT]
    return jnp.concatenate(
        [
            lower_half * cosine - upper_half * sine_part,
            upper_half * cosine + lower_half * sine_part,
            vectors[..., ROT:],
        ],
        axis=-1,
    )


def token_positions(local_req, cached):
    onehot = local_req[:, None] == jnp.arange(cached.shape[0], dtype=jnp.int32)[None, :]
    stretch_sizes = jnp.sum(onehot.astype(jnp.int32), axis=0)
    starts = jnp.cumsum(stretch_sizes) - stretch_sizes
    own_start = jnp.sum(jnp.where(onehot, starts[None, :], 0), axis=1)
    own_cached = jnp.sum(jnp.where(onehot, cached[None, :], 0), axis=1)
    return own_cached + jnp.arange(local_req.shape[0], dtype=jnp.int32) - own_start


def attend(queries, new_keys, new_values, cache_keys, cache_values, local_req, cached, positions):
    span = cache_keys.shape[0] // cached.shape[0]
    key_slot = jnp.arange(cache_keys.shape[0], dtype=jnp.int32)
    key_owner = key_slot // span
    key_place = key_slot % span
    cache_ok = (local_req[:, None] == key_owner[None, :]) & (
        key_place[None, :] < jnp.repeat(cached, span)[None, :]
    )
    new_ok = (local_req[:, None] == local_req[None, :]) & (positions[None, :] <= positions[:, None])
    allowed = jnp.concatenate([cache_ok, new_ok], axis=1)
    all_keys = jnp.concatenate([cache_keys, new_keys], axis=0)
    all_values = jnp.concatenate([cache_values, new_values], axis=0)
    scores = jnp.einsum(
        "thd,khd->htk", queries, all_keys, preferred_element_type=jnp.float32
    ) * HD ** (-0.5)
    scores = jnp.where(allowed[None], scores, -1e30)
    peak = jnp.max(scores, axis=2, keepdims=True)
    exp_scores = jnp.exp(scores - peak)
    attn_probs = (exp_scores / jnp.sum(exp_scores, axis=2, keepdims=True)).astype(jnp.bfloat16)
    return jnp.einsum(
        "htk,khd->thd", attn_probs, all_values, preferred_element_type=jnp.float32
    ).astype(jnp.bfloat16)


def share_pages(local_pool, groups):
    grouped = local_pool.reshape(
        local_pool.shape[0], 2, local_pool.shape[2], groups, local_pool.shape[3] // groups
    )
    shared = lax.all_to_all(grouped, "head", split_axis=3, concat_axis=0, tiled=True)
    return shared.reshape(shared.shape[0], 2, shared.shape[2], shared.shape[4])


def gather_by_all_to_all(block, axis):
    count = lax.axis_size(axis)
    copies = jnp.broadcast_to(block[None], (count,) + block.shape).reshape(
        (count * block.shape[0],) + block.shape[1:]
    )
    return lax.all_to_all(copies, axis, split_axis=0, concat_axis=0, tiled=True)


def shards(
    states,
    pre_gain,
    pre_shift,
    mlp_gain,
    mlp_shift,
    qkv_weight,
    qkv_bias,
    out_weight,
    out_bias,
    up_weight,
    up_bias,
    down_weight,
    down_bias,
    kv_cache,
    token_request,
    cached_len,
    page_table,
    migrations,
):
    gathered = lax.all_gather(states, "head", axis=1, tiled=True)
    qkv_full = gather_by_all_to_all(qkv_weight, "tok")
    out_full = lax.all_gather(out_weight, "tok", axis=1, tiled=True)
    wide = gathered.astype(jnp.float32)
    pre_normed = layer_norm(wide, pre_gain, pre_shift)
    mlp_normed = layer_norm(wide, mlp_gain, mlp_shift)
    tok_rows = gathered.shape[0]

    def feed(normed):
        hidden = jax.nn.gelu(
            jnp.dot(normed, up_weight, preferred_element_type=jnp.float32) + up_bias,
            approximate=False,
        ).astype(jnp.bfloat16)
        return jnp.dot(hidden, down_weight, preferred_element_type=jnp.float32)

    feed_part = feed(mlp_normed)
    kv_cache, feed_part = lax.optimization_barrier((kv_cache, feed_part))
    page_pool = share_pages(kv_cache, lax.axis_size("head"))
    joined = jnp.dot(pre_normed, qkv_full, preferred_element_type=jnp.float32)
    joined = (joined + qkv_bias).reshape(tok_rows, -1, 3, HD)
    local_req = token_request - lax.axis_index("tok") * cached_len.shape[0]
    positions = token_positions(local_req, cached_len)
    queries = rotate(joined[:, :, 0], positions).astype(jnp.bfloat16)
    new_keys = rotate(joined[:, :, 1], positions).astype(jnp.bfloat16)
    new_values = joined[:, :, 2].astype(jnp.bfloat16)
    sources = migrations[:, 0]
    targets = migrations[:, 1]
    table = page_table.reshape(-1)
    match = table[:, None] == targets[None, :]
    moved_from = jnp.sum(jnp.where(match, sources[None, :], 0), axis=1)
    table = jnp.where(jnp.any(match, axis=1), moved_from, table)
    pages = page_pool[table]
    cache_keys = pages[:, 0].reshape(-1, queries.shape[1], HD)
    cache_values = pages[:, 1].reshape(-1, queries.shape[1], HD)
    heads_out = attend(
        queries, new_keys, new_values, cache_keys, cache_values, local_req, cached_len, positions
    ).reshape(tok_rows, -1)
    attention_part = jnp.dot(heads_out, out_full, preferred_element_type=jnp.float32)
    summed = lax.psum_scatter(
        (attention_part + feed_part).astype(jnp.bfloat16), "head", scatter_dimension=1, tiled=True
    ).astype(jnp.float32)
    return (summed + out_bias + down_bias).astype(jnp.bfloat16)


def solution(mesh):
    in_specs = (
        P("tok", "head"),
        P(),
        P(),
        P(),
        P(),
        P("tok", "head"),
        P("head"),
        P("head", "tok"),
        P("head"),
        P(None, "head"),
        P("head"),
        P("head", None),
        P("head"),
        P(("tok", "head"), None, None, None),
        P("tok"),
        P("tok"),
        P("tok", None),
        P("tok", None),
    )
    out_specs = P("tok", "head")
    return jax.shard_map(shards, mesh=mesh, in_specs=in_specs, out_specs=out_specs, check_vma=False)
```

```python
import jax
import jax.numpy as jnp
from jax import lax
from jax.sharding import PartitionSpec as P

HD = 128
ROT = 32


epsilon = 1e-05


def layer_norm(wide, gain, shift):
    row_mean = jnp.mean(wide, axis=1, keepdims=True)
    centred = wide - row_mean
    row_var = jnp.mean(centred * centred, axis=1, keepdims=True)
    return (centred * lax.rsqrt(row_var + epsilon) * gain + shift).astype(jnp.bfloat16)


def rotate(vectors, positions):
    half_rot = ROT // 2
    inv_freq = 10000.0 ** (-2.0 * jnp.arange(half_rot, dtype=jnp.float32) / ROT)
    angles = positions.astype(jnp.float32)[:, None] * inv_freq[None, :]
    cosine = jnp.cos(angles)[:, None, :]
    sine_part = jnp.sin(angles)[:, None, :]
    lower_half = vectors[..., :half_rot]
    upper_half = vectors[..., half_rot:ROT]
    return jnp.concatenate(
        [
            lower_half * cosine - upper_half * sine_part,
            upper_half * cosine + lower_half * sine_part,
            vectors[..., ROT:],
        ],
        axis=-1,
    )


def token_positions(local_req, cached):
    onehot = local_req[:, None] == jnp.arange(cached.shape[0], dtype=jnp.int32)[None, :]
    stretch_sizes = jnp.sum(onehot.astype(jnp.int32), axis=0)
    starts = jnp.cumsum(stretch_sizes) - stretch_sizes
    own_start = jnp.sum(jnp.where(onehot, starts[None, :], 0), axis=1)
    own_cached = jnp.sum(jnp.where(onehot, cached[None, :], 0), axis=1)
    return own_cached + jnp.arange(local_req.shape[0], dtype=jnp.int32) - own_start


def attend(queries, new_keys, new_values, cache_keys, cache_values, local_req, cached, positions):
    span = cache_keys.shape[0] // cached.shape[0]
    key_slot = jnp.arange(cache_keys.shape[0], dtype=jnp.int32)
    key_owner = key_slot // span
    key_place = key_slot % span
    cache_ok = (local_req[:, None] == key_owner[None, :]) & (
        key_place[None, :] < jnp.repeat(cached, span)[None, :]
    )
    new_ok = (local_req[:, None] == local_req[None, :]) & (positions[None, :] <= positions[:, None])
    allowed = jnp.concatenate([cache_ok, new_ok], axis=1)
    all_keys = jnp.concatenate([cache_keys, new_keys], axis=0)
    all_values = jnp.concatenate([cache_values, new_values], axis=0)
    scores = jnp.einsum(
        "thd,khd->htk", queries, all_keys, preferred_element_type=jnp.float32
    ) * HD ** (-0.5)
    scores = jnp.where(allowed[None], scores, -1e30)
    peak = jnp.max(scores, axis=2, keepdims=True)
    exp_scores = jnp.exp(scores - peak)
    attn_probs = (exp_scores / jnp.sum(exp_scores, axis=2, keepdims=True)).astype(jnp.bfloat16)
    return jnp.einsum(
        "htk,khd->thd", attn_probs, all_values, preferred_element_type=jnp.float32
    ).astype(jnp.bfloat16)


def share_pages(local_pool, groups):
    grouped = local_pool.reshape(
        local_pool.shape[0], 2, local_pool.shape[2], groups, local_pool.shape[3] // groups
    )
    shared = lax.all_to_all(grouped, "head", split_axis=3, concat_axis=0, tiled=True)
    return shared.reshape(shared.shape[0], 2, shared.shape[2], shared.shape[4])


def gather_by_all_to_all(block, axis):
    count = lax.axis_size(axis)
    copies = jnp.broadcast_to(block[None], (count,) + block.shape).reshape(
        (count * block.shape[0],) + block.shape[1:]
    )
    return lax.all_to_all(copies, axis, split_axis=0, concat_axis=0, tiled=True)


def shards(
    states,
    pre_gain,
    pre_shift,
    mlp_gain,
    mlp_shift,
    qkv_weight,
    qkv_bias,
    out_weight,
    out_bias,
    up_weight,
    up_bias,
    down_weight,
    down_bias,
    kv_cache,
    token_request,
    cached_len,
    page_table,
    migrations,
):
    gathered = lax.all_gather(states, "head", axis=1, tiled=True)
    qkv_full = gather_by_all_to_all(qkv_weight, "tok")
    wide = gathered.astype(jnp.float32)
    pre_normed = layer_norm(wide, pre_gain, pre_shift)
    mlp_normed = layer_norm(wide, mlp_gain, mlp_shift)
    tok_rows = gathered.shape[0]

    def feed(normed):
        hidden = jax.nn.gelu(
            jnp.dot(normed, up_weight, preferred_element_type=jnp.float32) + up_bias,
            approximate=False,
        ).astype(jnp.bfloat16)
        return jnp.dot(hidden, down_weight, preferred_element_type=jnp.float32)

    feed_part = feed(mlp_normed)
    kv_cache, feed_part, out_weight, qkv_full = lax.optimization_barrier(
        (kv_cache, feed_part, out_weight, qkv_full)
    )
    out_full = lax.all_gather(out_weight, "tok", axis=1, tiled=True)
    page_pool = share_pages(kv_cache, lax.axis_size("head"))
    joined = jnp.dot(pre_normed, qkv_full, preferred_element_type=jnp.float32)
    joined = (joined + qkv_bias).reshape(tok_rows, -1, 3, HD)
    local_req = token_request - lax.axis_index("tok") * cached_len.shape[0]
    positions = token_positions(local_req, cached_len)
    queries = rotate(joined[:, :, 0], positions).astype(jnp.bfloat16)
    new_keys = rotate(joined[:, :, 1], positions).astype(jnp.bfloat16)
    new_values = joined[:, :, 2].astype(jnp.bfloat16)
    sources = migrations[:, 0]
    targets = migrations[:, 1]
    table = page_table.reshape(-1)
    match = table[:, None] == targets[None, :]
    moved_from = jnp.sum(jnp.where(match, sources[None, :], 0), axis=1)
    table = jnp.where(jnp.any(match, axis=1), moved_from, table)
    pages = page_pool[table]
    cache_keys = pages[:, 0].reshape(-1, queries.shape[1], HD)
    cache_values = pages[:, 1].reshape(-1, queries.shape[1], HD)
    heads_out = attend(
        queries, new_keys, new_values, cache_keys, cache_values, local_req, cached_len, positions
    ).reshape(tok_rows, -1)
    attention_part = jnp.dot(heads_out, out_full, preferred_element_type=jnp.float32)
    summed = lax.psum_scatter(
        (attention_part + feed_part).astype(jnp.bfloat16), "head", scatter_dimension=1, tiled=True
    ).astype(jnp.float32)
    return (summed + out_bias + down_bias).astype(jnp.bfloat16)


def solution(mesh):
    in_specs = (
        P("tok", "head"),
        P(),
        P(),
        P(),
        P(),
        P("tok", "head"),
        P("head"),
        P("head", "tok"),
        P("head"),
        P(None, "head"),
        P("head"),
        P("head", None),
        P("head"),
        P(("tok", "head"), None, None, None),
        P("tok"),
        P("tok"),
        P("tok", None),
        P("tok", None),
    )
    out_specs = P("tok", "head")
    return jax.shard_map(shards, mesh=mesh, in_specs=in_specs, out_specs=out_specs, check_vma=False)
```

```python
import jax
import jax.numpy as jnp
from jax import lax
from jax.sharding import PartitionSpec as P

HD = 128
ROT = 32


epsilon = 1e-05


def layer_norm(wide, gain, shift):
    row_mean = jnp.mean(wide, axis=1, keepdims=True)
    centred = wide - row_mean
    row_var = jnp.mean(centred * centred, axis=1, keepdims=True)
    return (centred * lax.rsqrt(row_var + epsilon) * gain + shift).astype(jnp.bfloat16)


def rotate(vectors, positions):
    half_rot = ROT // 2
    inv_freq = 10000.0 ** (-2.0 * jnp.arange(half_rot, dtype=jnp.float32) / ROT)
    angles = positions.astype(jnp.float32)[:, None] * inv_freq[None, :]
    cosine = jnp.cos(angles)[:, None, :]
    sine_part = jnp.sin(angles)[:, None, :]
    lower_half = vectors[..., :half_rot]
    upper_half = vectors[..., half_rot:ROT]
    return jnp.concatenate(
        [
            lower_half * cosine - upper_half * sine_part,
            upper_half * cosine + lower_half * sine_part,
            vectors[..., ROT:],
        ],
        axis=-1,
    )


def token_positions(local_req, cached):
    onehot = local_req[:, None] == jnp.arange(cached.shape[0], dtype=jnp.int32)[None, :]
    stretch_sizes = jnp.sum(onehot.astype(jnp.int32), axis=0)
    starts = jnp.cumsum(stretch_sizes) - stretch_sizes
    own_start = jnp.sum(jnp.where(onehot, starts[None, :], 0), axis=1)
    own_cached = jnp.sum(jnp.where(onehot, cached[None, :], 0), axis=1)
    return own_cached + jnp.arange(local_req.shape[0], dtype=jnp.int32) - own_start


def attend(queries, new_keys, new_values, cache_keys, cache_values, local_req, cached, positions):
    span = cache_keys.shape[0] // cached.shape[0]
    key_slot = jnp.arange(cache_keys.shape[0], dtype=jnp.int32)
    key_owner = key_slot // span
    key_place = key_slot % span
    cache_ok = (local_req[:, None] == key_owner[None, :]) & (
        key_place[None, :] < jnp.repeat(cached, span)[None, :]
    )
    new_ok = (local_req[:, None] == local_req[None, :]) & (positions[None, :] <= positions[:, None])
    allowed = jnp.concatenate([cache_ok, new_ok], axis=1)
    all_keys = jnp.concatenate([cache_keys, new_keys], axis=0)
    all_values = jnp.concatenate([cache_values, new_values], axis=0)
    scores = jnp.einsum(
        "thd,khd->htk", queries, all_keys, preferred_element_type=jnp.float32
    ) * HD ** (-0.5)
    scores = jnp.where(allowed[None], scores, -1e30)
    peak = jnp.max(scores, axis=2, keepdims=True)
    exp_scores = jnp.exp(scores - peak)
    attn_probs = (exp_scores / jnp.sum(exp_scores, axis=2, keepdims=True)).astype(jnp.bfloat16)
    return jnp.einsum(
        "htk,khd->thd", attn_probs, all_values, preferred_element_type=jnp.float32
    ).astype(jnp.bfloat16)


def share_pages(local_pool, groups):
    grouped = local_pool.reshape(
        local_pool.shape[0], 2, local_pool.shape[2], groups, local_pool.shape[3] // groups
    )
    shared = lax.all_to_all(grouped, "head", split_axis=3, concat_axis=0, tiled=True)
    return shared.reshape(shared.shape[0], 2, shared.shape[2], shared.shape[4])


def gather_by_all_to_all(block, axis):
    count = lax.axis_size(axis)
    copies = jnp.broadcast_to(block[None], (count,) + block.shape).reshape(
        (count * block.shape[0],) + block.shape[1:]
    )
    return lax.all_to_all(copies, axis, split_axis=0, concat_axis=0, tiled=True)


def share_pages_by_permutes(local_pool):
    count = lax.axis_size("head")
    me = lax.axis_index("head")
    width = local_pool.shape[3] // count
    received = [lax.dynamic_slice_in_dim(local_pool, me * width, width, axis=3)]
    for shift in range(1, count):
        part = lax.dynamic_slice_in_dim(local_pool, ((me + shift) % count) * width, width, axis=3)
        perm = [(i, (i + shift) % count) for i in range(count)]
        received.append(lax.ppermute(part, "head", perm))
    owners = jnp.arange(count, dtype=jnp.int32)
    return jnp.concatenate(received, axis=0), (me - owners) % count


def shards(
    states,
    pre_gain,
    pre_shift,
    mlp_gain,
    mlp_shift,
    qkv_weight,
    qkv_bias,
    out_weight,
    out_bias,
    up_weight,
    up_bias,
    down_weight,
    down_bias,
    kv_cache,
    token_request,
    cached_len,
    page_table,
    migrations,
):
    gathered = lax.all_gather(states, "head", axis=1, tiled=True)
    page_pool, pool_order = share_pages_by_permutes(kv_cache)
    qkv_full = gather_by_all_to_all(qkv_weight, "tok")
    out_full = lax.all_gather(out_weight, "tok", axis=1, tiled=True)
    wide = gathered.astype(jnp.float32)
    pre_normed = layer_norm(wide, pre_gain, pre_shift)
    mlp_normed = layer_norm(wide, mlp_gain, mlp_shift)
    tok_rows = gathered.shape[0]

    def feed(normed):
        hidden = jax.nn.gelu(
            jnp.dot(normed, up_weight, preferred_element_type=jnp.float32) + up_bias,
            approximate=False,
        ).astype(jnp.bfloat16)
        return jnp.dot(hidden, down_weight, preferred_element_type=jnp.float32)

    feed_part = feed(mlp_normed)
    joined = jnp.dot(pre_normed, qkv_full, preferred_element_type=jnp.float32)
    joined = (joined + qkv_bias).reshape(tok_rows, -1, 3, HD)
    local_req = token_request - lax.axis_index("tok") * cached_len.shape[0]
    positions = token_positions(local_req, cached_len)
    queries = rotate(joined[:, :, 0], positions).astype(jnp.bfloat16)
    new_keys = rotate(joined[:, :, 1], positions).astype(jnp.bfloat16)
    new_values = joined[:, :, 2].astype(jnp.bfloat16)
    sources = migrations[:, 0]
    targets = migrations[:, 1]
    table = page_table.reshape(-1)
    match = table[:, None] == targets[None, :]
    moved_from = jnp.sum(jnp.where(match, sources[None, :], 0), axis=1)
    table = jnp.where(jnp.any(match, axis=1), moved_from, table)
    slots = kv_cache.shape[0]
    pages = page_pool[pool_order[table // slots] * slots + table % slots]
    cache_keys = pages[:, 0].reshape(-1, queries.shape[1], HD)
    cache_values = pages[:, 1].reshape(-1, queries.shape[1], HD)
    heads_out = attend(
        queries, new_keys, new_values, cache_keys, cache_values, local_req, cached_len, positions
    ).reshape(tok_rows, -1)
    attention_part = jnp.dot(heads_out, out_full, preferred_element_type=jnp.float32)
    summed = lax.psum_scatter(
        (attention_part + feed_part).astype(jnp.bfloat16), "head", scatter_dimension=1, tiled=True
    ).astype(jnp.float32)
    return (summed + out_bias + down_bias).astype(jnp.bfloat16)


def solution(mesh):
    in_specs = (
        P("tok", "head"),
        P(),
        P(),
        P(),
        P(),
        P("tok", "head"),
        P("head"),
        P("head", "tok"),
        P("head"),
        P(None, "head"),
        P("head"),
        P("head", None),
        P("head"),
        P(("tok", "head"), None, None, None),
        P("tok"),
        P("tok"),
        P("tok", None),
        P("tok", None),
    )
    out_specs = P("tok", "head")
    return jax.shard_map(shards, mesh=mesh, in_specs=in_specs, out_specs=out_specs, check_vma=False)
```

```python
import jax
import jax.numpy as jnp
from jax import lax
from jax.sharding import PartitionSpec as P

HD = 128
ROT = 32


epsilon = 1e-05


def layer_norm(wide, gain, shift):
    row_mean = jnp.mean(wide, axis=1, keepdims=True)
    centred = wide - row_mean
    row_var = jnp.mean(centred * centred, axis=1, keepdims=True)
    return (centred * lax.rsqrt(row_var + epsilon) * gain + shift).astype(jnp.bfloat16)


def rotate(vectors, positions):
    half_rot = ROT // 2
    inv_freq = 10000.0 ** (-2.0 * jnp.arange(half_rot, dtype=jnp.float32) / ROT)
    angles = positions.astype(jnp.float32)[:, None] * inv_freq[None, :]
    cosine = jnp.cos(angles)[:, None, :]
    sine_part = jnp.sin(angles)[:, None, :]
    lower_half = vectors[..., :half_rot]
    upper_half = vectors[..., half_rot:ROT]
    return jnp.concatenate(
        [
            lower_half * cosine - upper_half * sine_part,
            upper_half * cosine + lower_half * sine_part,
            vectors[..., ROT:],
        ],
        axis=-1,
    )


def token_positions(local_req, cached):
    onehot = local_req[:, None] == jnp.arange(cached.shape[0], dtype=jnp.int32)[None, :]
    stretch_sizes = jnp.sum(onehot.astype(jnp.int32), axis=0)
    starts = jnp.cumsum(stretch_sizes) - stretch_sizes
    own_start = jnp.sum(jnp.where(onehot, starts[None, :], 0), axis=1)
    own_cached = jnp.sum(jnp.where(onehot, cached[None, :], 0), axis=1)
    return own_cached + jnp.arange(local_req.shape[0], dtype=jnp.int32) - own_start


def attend(queries, new_keys, new_values, cache_keys, cache_values, local_req, cached, positions):
    span = cache_keys.shape[0] // cached.shape[0]
    key_slot = jnp.arange(cache_keys.shape[0], dtype=jnp.int32)
    key_owner = key_slot // span
    key_place = key_slot % span
    cache_ok = (local_req[:, None] == key_owner[None, :]) & (
        key_place[None, :] < jnp.repeat(cached, span)[None, :]
    )
    new_ok = (local_req[:, None] == local_req[None, :]) & (positions[None, :] <= positions[:, None])
    allowed = jnp.concatenate([cache_ok, new_ok], axis=1)
    all_keys = jnp.concatenate([cache_keys, new_keys], axis=0)
    all_values = jnp.concatenate([cache_values, new_values], axis=0)
    scores = jnp.einsum(
        "thd,khd->htk", queries, all_keys, preferred_element_type=jnp.float32
    ) * HD ** (-0.5)
    scores = jnp.where(allowed[None], scores, -1e30)
    peak = jnp.max(scores, axis=2, keepdims=True)
    exp_scores = jnp.exp(scores - peak)
    attn_probs = (exp_scores / jnp.sum(exp_scores, axis=2, keepdims=True)).astype(jnp.bfloat16)
    return jnp.einsum(
        "htk,khd->thd", attn_probs, all_values, preferred_element_type=jnp.float32
    ).astype(jnp.bfloat16)


def share_pages(local_pool, groups):
    grouped = local_pool.reshape(
        local_pool.shape[0], 2, local_pool.shape[2], groups, local_pool.shape[3] // groups
    )
    shared = lax.all_to_all(grouped, "head", split_axis=3, concat_axis=0, tiled=True)
    return shared.reshape(shared.shape[0], 2, shared.shape[2], shared.shape[4])


def gather_by_all_to_all(block, axis):
    count = lax.axis_size(axis)
    copies = jnp.broadcast_to(block[None], (count,) + block.shape).reshape(
        (count * block.shape[0],) + block.shape[1:]
    )
    return lax.all_to_all(copies, axis, split_axis=0, concat_axis=0, tiled=True)


def share_pages_by_permutes(local_pool):
    count = lax.axis_size("head")
    me = lax.axis_index("head")
    width = local_pool.shape[3] // count
    received = [lax.dynamic_slice_in_dim(local_pool, me * width, width, axis=3)]
    for shift in range(1, count):
        part = lax.dynamic_slice_in_dim(local_pool, ((me + shift) % count) * width, width, axis=3)
        perm = [(i, (i + shift) % count) for i in range(count)]
        received.append(lax.ppermute(part, "head", perm))
    owners = jnp.arange(count, dtype=jnp.int32)
    return jnp.concatenate(received, axis=0), (me - owners) % count


def shards(
    states,
    pre_gain,
    pre_shift,
    mlp_gain,
    mlp_shift,
    qkv_weight,
    qkv_bias,
    out_weight,
    out_bias,
    up_weight,
    up_bias,
    down_weight,
    down_bias,
    kv_cache,
    token_request,
    cached_len,
    page_table,
    migrations,
):
    gathered = lax.all_gather(states, "head", axis=1, tiled=True)
    qkv_full = gather_by_all_to_all(qkv_weight, "tok")
    out_full = lax.all_gather(out_weight, "tok", axis=1, tiled=True)
    wide = gathered.astype(jnp.float32)
    pre_normed = layer_norm(wide, pre_gain, pre_shift)
    mlp_normed = layer_norm(wide, mlp_gain, mlp_shift)
    tok_rows = gathered.shape[0]

    def feed(normed):
        hidden = jax.nn.gelu(
            jnp.dot(normed, up_weight, preferred_element_type=jnp.float32) + up_bias,
            approximate=False,
        ).astype(jnp.bfloat16)
        return jnp.dot(hidden, down_weight, preferred_element_type=jnp.float32)

    feed_part = feed(mlp_normed)
    kv_cache, feed_part = lax.optimization_barrier((kv_cache, feed_part))
    page_pool, pool_order = share_pages_by_permutes(kv_cache)
    qkv_full, page_pool = lax.optimization_barrier((qkv_full, page_pool))
    joined = jnp.dot(pre_normed, qkv_full, preferred_element_type=jnp.float32)
    joined = (joined + qkv_bias).reshape(tok_rows, -1, 3, HD)
    local_req = token_request - lax.axis_index("tok") * cached_len.shape[0]
    positions = token_positions(local_req, cached_len)
    queries = rotate(joined[:, :, 0], positions).astype(jnp.bfloat16)
    new_keys = rotate(joined[:, :, 1], positions).astype(jnp.bfloat16)
    new_values = joined[:, :, 2].astype(jnp.bfloat16)
    sources = migrations[:, 0]
    targets = migrations[:, 1]
    table = page_table.reshape(-1)
    match = table[:, None] == targets[None, :]
    moved_from = jnp.sum(jnp.where(match, sources[None, :], 0), axis=1)
    table = jnp.where(jnp.any(match, axis=1), moved_from, table)
    slots = kv_cache.shape[0]
    pages = page_pool[pool_order[table // slots] * slots + table % slots]
    cache_keys = pages[:, 0].reshape(-1, queries.shape[1], HD)
    cache_values = pages[:, 1].reshape(-1, queries.shape[1], HD)
    heads_out = attend(
        queries, new_keys, new_values, cache_keys, cache_values, local_req, cached_len, positions
    ).reshape(tok_rows, -1)
    attention_part = jnp.dot(heads_out, out_full, preferred_element_type=jnp.float32)
    summed = lax.psum_scatter(
        (attention_part + feed_part).astype(jnp.bfloat16), "head", scatter_dimension=1, tiled=True
    ).astype(jnp.float32)
    return (summed + out_bias + down_bias).astype(jnp.bfloat16)


def solution(mesh):
    in_specs = (
        P("tok", "head"),
        P(),
        P(),
        P(),
        P(),
        P("tok", "head"),
        P("head"),
        P("head", "tok"),
        P("head"),
        P(None, "head"),
        P("head"),
        P("head", None),
        P("head"),
        P(("tok", "head"), None, None, None),
        P("tok"),
        P("tok"),
        P("tok", None),
        P("tok", None),
    )
    out_specs = P("tok", "head")
    return jax.shard_map(shards, mesh=mesh, in_specs=in_specs, out_specs=out_specs, check_vma=False)
```

```python
import jax
import jax.numpy as jnp
from jax import lax
from jax.sharding import PartitionSpec as P

HD = 128
ROT = 32


epsilon = 1e-05


def layer_norm(wide, gain, shift):
    row_mean = jnp.mean(wide, axis=1, keepdims=True)
    centred = wide - row_mean
    row_var = jnp.mean(centred * centred, axis=1, keepdims=True)
    return (centred * lax.rsqrt(row_var + epsilon) * gain + shift).astype(jnp.bfloat16)


def rotate(vectors, positions):
    half_rot = ROT // 2
    inv_freq = 10000.0 ** (-2.0 * jnp.arange(half_rot, dtype=jnp.float32) / ROT)
    angles = positions.astype(jnp.float32)[:, None] * inv_freq[None, :]
    cosine = jnp.cos(angles)[:, None, :]
    sine_part = jnp.sin(angles)[:, None, :]
    lower_half = vectors[..., :half_rot]
    upper_half = vectors[..., half_rot:ROT]
    return jnp.concatenate(
        [
            lower_half * cosine - upper_half * sine_part,
            upper_half * cosine + lower_half * sine_part,
            vectors[..., ROT:],
        ],
        axis=-1,
    )


def token_positions(local_req, cached):
    onehot = local_req[:, None] == jnp.arange(cached.shape[0], dtype=jnp.int32)[None, :]
    stretch_sizes = jnp.sum(onehot.astype(jnp.int32), axis=0)
    starts = jnp.cumsum(stretch_sizes) - stretch_sizes
    own_start = jnp.sum(jnp.where(onehot, starts[None, :], 0), axis=1)
    own_cached = jnp.sum(jnp.where(onehot, cached[None, :], 0), axis=1)
    return own_cached + jnp.arange(local_req.shape[0], dtype=jnp.int32) - own_start


def attend(queries, new_keys, new_values, cache_keys, cache_values, local_req, cached, positions):
    span = cache_keys.shape[0] // cached.shape[0]
    key_slot = jnp.arange(cache_keys.shape[0], dtype=jnp.int32)
    key_owner = key_slot // span
    key_place = key_slot % span
    cache_ok = (local_req[:, None] == key_owner[None, :]) & (
        key_place[None, :] < jnp.repeat(cached, span)[None, :]
    )
    new_ok = (local_req[:, None] == local_req[None, :]) & (positions[None, :] <= positions[:, None])
    allowed = jnp.concatenate([cache_ok, new_ok], axis=1)
    all_keys = jnp.concatenate([cache_keys, new_keys], axis=0)
    all_values = jnp.concatenate([cache_values, new_values], axis=0)
    scores = jnp.einsum(
        "thd,khd->htk", queries, all_keys, preferred_element_type=jnp.float32
    ) * HD ** (-0.5)
    scores = jnp.where(allowed[None], scores, -1e30)
    peak = jnp.max(scores, axis=2, keepdims=True)
    exp_scores = jnp.exp(scores - peak)
    attn_probs = (exp_scores / jnp.sum(exp_scores, axis=2, keepdims=True)).astype(jnp.bfloat16)
    return jnp.einsum(
        "htk,khd->thd", attn_probs, all_values, preferred_element_type=jnp.float32
    ).astype(jnp.bfloat16)


def share_pages(local_pool, groups):
    grouped = local_pool.reshape(
        local_pool.shape[0], 2, local_pool.shape[2], groups, local_pool.shape[3] // groups
    )
    shared = lax.all_to_all(grouped, "head", split_axis=3, concat_axis=0, tiled=True)
    return shared.reshape(shared.shape[0], 2, shared.shape[2], shared.shape[4])


def gather_by_all_to_all(block, axis):
    count = lax.axis_size(axis)
    copies = jnp.broadcast_to(block[None], (count,) + block.shape).reshape(
        (count * block.shape[0],) + block.shape[1:]
    )
    return lax.all_to_all(copies, axis, split_axis=0, concat_axis=0, tiled=True)


def shards(
    states,
    pre_gain,
    pre_shift,
    mlp_gain,
    mlp_shift,
    qkv_weight,
    qkv_bias,
    out_weight,
    out_bias,
    up_weight,
    up_bias,
    down_weight,
    down_bias,
    kv_cache,
    token_request,
    cached_len,
    page_table,
    migrations,
):
    gathered = lax.all_gather(states, "head", axis=1, tiled=True)
    split = qkv_weight.shape[1] // 2
    qkv_first = gather_by_all_to_all(qkv_weight[:, :split], "tok")
    qkv_second, gathered = lax.optimization_barrier((qkv_weight[:, split:], gathered))
    qkv_second = lax.all_gather(qkv_second, "tok", axis=0, tiled=True)
    wide = gathered.astype(jnp.float32)
    pre_normed = layer_norm(wide, pre_gain, pre_shift)
    mlp_normed = layer_norm(wide, mlp_gain, mlp_shift)
    tok_rows = gathered.shape[0]

    def feed(normed):
        hidden = jax.nn.gelu(
            jnp.dot(normed, up_weight, preferred_element_type=jnp.float32) + up_bias,
            approximate=False,
        ).astype(jnp.bfloat16)
        return jnp.dot(hidden, down_weight, preferred_element_type=jnp.float32)

    feed_part = feed(mlp_normed)
    kv_cache, feed_part = lax.optimization_barrier((kv_cache, feed_part))
    page_pool = share_pages(kv_cache, lax.axis_size("head"))
    out_weight, page_pool = lax.optimization_barrier((out_weight, page_pool))
    out_blocks = gather_by_all_to_all(out_weight, "tok").reshape(
        (lax.axis_size("tok"),) + out_weight.shape
    )
    joined = jnp.concatenate(
        [
            jnp.dot(pre_normed, qkv_first, preferred_element_type=jnp.float32),
            jnp.dot(pre_normed, qkv_second, preferred_element_type=jnp.float32),
        ],
        axis=1,
    )
    joined = (joined + qkv_bias).reshape(tok_rows, -1, 3, HD)
    local_req = token_request - lax.axis_index("tok") * cached_len.shape[0]
    positions = token_positions(local_req, cached_len)
    queries = rotate(joined[:, :, 0], positions).astype(jnp.bfloat16)
    new_keys = rotate(joined[:, :, 1], positions).astype(jnp.bfloat16)
    new_values = joined[:, :, 2].astype(jnp.bfloat16)
    sources = migrations[:, 0]
    targets = migrations[:, 1]
    table = page_table.reshape(-1)
    match = table[:, None] == targets[None, :]
    moved_from = jnp.sum(jnp.where(match, sources[None, :], 0), axis=1)
    table = jnp.where(jnp.any(match, axis=1), moved_from, table)
    pages = page_pool[table]
    cache_keys = pages[:, 0].reshape(-1, queries.shape[1], HD)
    cache_values = pages[:, 1].reshape(-1, queries.shape[1], HD)
    heads_out = attend(
        queries, new_keys, new_values, cache_keys, cache_values, local_req, cached_len, positions
    ).reshape(tok_rows, -1)
    attention_part = jnp.einsum(
        "td,bdc->tbc", heads_out, out_blocks, preferred_element_type=jnp.float32
    ).reshape(tok_rows, -1)
    summed = lax.psum_scatter(
        (attention_part + feed_part).astype(jnp.bfloat16), "head", scatter_dimension=1, tiled=True
    ).astype(jnp.float32)
    return (summed + out_bias + down_bias).astype(jnp.bfloat16)


def solution(mesh):
    in_specs = (
        P("tok", "head"),
        P(),
        P(),
        P(),
        P(),
        P("tok", "head"),
        P("head"),
        P("head", "tok"),
        P("head"),
        P(None, "head"),
        P("head"),
        P("head", None),
        P("head"),
        P(("tok", "head"), None, None, None),
        P("tok"),
        P("tok"),
        P("tok", None),
        P("tok", None),
    )
    out_specs = P("tok", "head")
    return jax.shard_map(shards, mesh=mesh, in_specs=in_specs, out_specs=out_specs, check_vma=False)
```

```python
import jax
import jax.numpy as jnp
from jax import lax
from jax.sharding import PartitionSpec as P
from jax.experimental import pallas as pl
from jax.experimental.pallas import tpu as pltpu

HD = 128
ROT = 32


epsilon = 1e-05


def layer_norm(wide, gain, shift):
    row_mean = jnp.mean(wide, axis=1, keepdims=True)
    centred = wide - row_mean
    row_var = jnp.mean(centred * centred, axis=1, keepdims=True)
    return (centred * lax.rsqrt(row_var + epsilon) * gain + shift).astype(jnp.bfloat16)


def rotate(vectors, positions):
    half_rot = ROT // 2
    inv_freq = 10000.0 ** (-2.0 * jnp.arange(half_rot, dtype=jnp.float32) / ROT)
    angles = positions.astype(jnp.float32)[:, None] * inv_freq[None, :]
    cosine = jnp.cos(angles)[:, None, :]
    sine_part = jnp.sin(angles)[:, None, :]
    lower_half = vectors[..., :half_rot]
    upper_half = vectors[..., half_rot:ROT]
    return jnp.concatenate(
        [
            lower_half * cosine - upper_half * sine_part,
            upper_half * cosine + lower_half * sine_part,
            vectors[..., ROT:],
        ],
        axis=-1,
    )


def token_positions(local_req, cached):
    onehot = local_req[:, None] == jnp.arange(cached.shape[0], dtype=jnp.int32)[None, :]
    stretch_sizes = jnp.sum(onehot.astype(jnp.int32), axis=0)
    starts = jnp.cumsum(stretch_sizes) - stretch_sizes
    own_start = jnp.sum(jnp.where(onehot, starts[None, :], 0), axis=1)
    own_cached = jnp.sum(jnp.where(onehot, cached[None, :], 0), axis=1)
    return own_cached + jnp.arange(local_req.shape[0], dtype=jnp.int32) - own_start


def attend(queries, new_keys, new_values, cache_keys, cache_values, local_req, cached, positions):
    span = cache_keys.shape[0] // cached.shape[0]
    key_slot = jnp.arange(cache_keys.shape[0], dtype=jnp.int32)
    key_owner = key_slot // span
    key_place = key_slot % span
    cache_ok = (local_req[:, None] == key_owner[None, :]) & (
        key_place[None, :] < jnp.repeat(cached, span)[None, :]
    )
    new_ok = (local_req[:, None] == local_req[None, :]) & (positions[None, :] <= positions[:, None])
    allowed = jnp.concatenate([cache_ok, new_ok], axis=1)
    all_keys = jnp.concatenate([cache_keys, new_keys], axis=0)
    all_values = jnp.concatenate([cache_values, new_values], axis=0)
    scores = jnp.einsum(
        "thd,khd->htk", queries, all_keys, preferred_element_type=jnp.float32
    ) * HD ** (-0.5)
    scores = jnp.where(allowed[None], scores, -1e30)
    peak = jnp.max(scores, axis=2, keepdims=True)
    exp_scores = jnp.exp(scores - peak)
    attn_probs = (exp_scores / jnp.sum(exp_scores, axis=2, keepdims=True)).astype(jnp.bfloat16)
    return jnp.einsum(
        "htk,khd->thd", attn_probs, all_values, preferred_element_type=jnp.float32
    ).astype(jnp.bfloat16)


def attention_kernel(
    q_ref, kc_ref, vc_ref, kn_ref, vn_ref, req_col, pos_col, owner_row, limit_row, req_row, pos_row, o_ref
):
    queries = q_ref[...]
    cache_keys = kc_ref[...].reshape(-1, queries.shape[1])
    cache_values = vc_ref[...].reshape(-1, queries.shape[1])
    dims = (((1,), (1,)), ((), ()))
    scale = HD ** (-0.5)
    cache_scores = lax.dot_general(queries, cache_keys, dims, preferred_element_type=jnp.float32) * scale
    new_scores = lax.dot_general(queries, kn_ref[...], dims, preferred_element_type=jnp.float32) * scale
    cache_place = lax.broadcasted_iota(jnp.int32, cache_scores.shape, 1) % (
        cache_scores.shape[1] // 2
    )
    cache_ok = (req_col[...] == owner_row[...]) & (cache_place < limit_row[...])
    new_ok = (req_col[...] == req_row[...]) & (pos_row[...] <= pos_col[...])
    cache_scores = jnp.where(cache_ok, cache_scores, -1e30)
    new_scores = jnp.where(new_ok, new_scores, -1e30)
    peak = jnp.maximum(
        jnp.max(cache_scores, axis=1, keepdims=True), jnp.max(new_scores, axis=1, keepdims=True)
    )
    cache_exp = jnp.exp(cache_scores - peak)
    new_exp = jnp.exp(new_scores - peak)
    total = jnp.sum(cache_exp, axis=1, keepdims=True) + jnp.sum(new_exp, axis=1, keepdims=True)
    cache_probs = (cache_exp / total).astype(jnp.bfloat16)
    new_probs = (new_exp / total).astype(jnp.bfloat16)
    mixed = jnp.dot(cache_probs, cache_values, preferred_element_type=jnp.float32) + jnp.dot(
        new_probs, vn_ref[...], preferred_element_type=jnp.float32
    )
    o_ref[...] = mixed.astype(o_ref.dtype)


def attend_kernel(queries, new_keys, new_values, pages, local_req, cached, positions):
    tokens, heads = queries.shape[0], queries.shape[1]
    page_count, page_len = pages.shape[0], pages.shape[2]
    span = page_count * page_len // cached.shape[0]
    key_slot = jnp.arange(page_count * page_len, dtype=jnp.int32)
    owner_row = (key_slot // span)[None, :]
    limit_row = jnp.repeat(cached, span)[None, :]
    flat = lambda x: x.reshape(tokens, heads * HD)
    row_block = pl.BlockSpec((tokens, HD), lambda h: (0, h))
    page_block = lambda part: pl.BlockSpec((page_count, 1, page_len, HD), lambda h: (0, part, 0, h))
    whole = lambda x: pl.BlockSpec(x.shape, lambda h: (0,) * x.ndim)
    extras = (
        local_req[:, None],
        positions[:, None],
        owner_row,
        limit_row,
        local_req[None, :],
        positions[None, :],
    )
    keys_seen = page_count * page_len + tokens
    out = pl.pallas_call(
        attention_kernel,
        grid=(heads,),
        in_specs=[row_block, page_block(0), page_block(1), row_block, row_block]
        + [whole(x) for x in extras],
        out_specs=row_block,
        out_shape=jax.ShapeDtypeStruct((tokens, heads * HD), jnp.bfloat16),
        cost_estimate=pl.CostEstimate(
            flops=4 * heads * tokens * keys_seen * HD,
            transcendentals=heads * tokens * keys_seen,
            bytes_accessed=2 * HD * heads * (2 * tokens + 2 * keys_seen),
        ),
    )(flat(queries), pages, pages, flat(new_keys), flat(new_values), *extras)
    return out


def share_pages(local_pool, groups):
    grouped = local_pool.reshape(
        local_pool.shape[0], 2, local_pool.shape[2], groups, local_pool.shape[3] // groups
    )
    shared = lax.all_to_all(grouped, "head", split_axis=3, concat_axis=0, tiled=True)
    return shared.reshape(shared.shape[0], 2, shared.shape[2], shared.shape[4])


def gather_by_all_to_all(block, axis):
    count = lax.axis_size(axis)
    copies = jnp.broadcast_to(block[None], (count,) + block.shape).reshape(
        (count * block.shape[0],) + block.shape[1:]
    )
    return lax.all_to_all(copies, axis, split_axis=0, concat_axis=0, tiled=True)


def shards(
    states,
    pre_gain,
    pre_shift,
    mlp_gain,
    mlp_shift,
    qkv_weight,
    qkv_bias,
    out_weight,
    out_bias,
    up_weight,
    up_bias,
    down_weight,
    down_bias,
    kv_cache,
    token_request,
    cached_len,
    page_table,
    migrations,
):
    gathered = lax.all_gather(states, "head", axis=1, tiled=True)
    qkv_full = gather_by_all_to_all(qkv_weight, "tok")
    out_full = lax.all_gather(out_weight, "tok", axis=1, tiled=True)
    wide = gathered.astype(jnp.float32)
    pre_normed = layer_norm(wide, pre_gain, pre_shift)
    mlp_normed = layer_norm(wide, mlp_gain, mlp_shift)
    tok_rows = gathered.shape[0]

    def feed(normed):
        hidden = jax.nn.gelu(
            jnp.dot(normed, up_weight, preferred_element_type=jnp.float32) + up_bias,
            approximate=False,
        ).astype(jnp.bfloat16)
        return jnp.dot(hidden, down_weight, preferred_element_type=jnp.float32)

    feed_part = feed(mlp_normed)
    kv_cache, feed_part = lax.optimization_barrier((kv_cache, feed_part))
    page_pool = share_pages(kv_cache, lax.axis_size("head"))
    joined = jnp.dot(pre_normed, qkv_full, preferred_element_type=jnp.float32)
    joined = (joined + qkv_bias).reshape(tok_rows, -1, 3, HD)
    local_req = token_request - lax.axis_index("tok") * cached_len.shape[0]
    positions = token_positions(local_req, cached_len)
    queries = rotate(joined[:, :, 0], positions).astype(jnp.bfloat16)
    new_keys = rotate(joined[:, :, 1], positions).astype(jnp.bfloat16)
    new_values = joined[:, :, 2].astype(jnp.bfloat16)
    sources = migrations[:, 0]
    targets = migrations[:, 1]
    table = page_table.reshape(-1)
    match = table[:, None] == targets[None, :]
    moved_from = jnp.sum(jnp.where(match, sources[None, :], 0), axis=1)
    table = jnp.where(jnp.any(match, axis=1), moved_from, table)
    pages = page_pool[table]
    heads_out = attend_kernel(
        queries, new_keys, new_values, pages, local_req, cached_len, positions
    )
    attention_part = jnp.dot(heads_out, out_full, preferred_element_type=jnp.float32)
    summed = lax.psum_scatter(
        (attention_part + feed_part).astype(jnp.bfloat16), "head", scatter_dimension=1, tiled=True
    ).astype(jnp.float32)
    return (summed + out_bias + down_bias).astype(jnp.bfloat16)


def solution(mesh):
    in_specs = (
        P("tok", "head"),
        P(),
        P(),
        P(),
        P(),
        P("tok", "head"),
        P("head"),
        P("head", "tok"),
        P("head"),
        P(None, "head"),
        P("head"),
        P("head", None),
        P("head"),
        P(("tok", "head"), None, None, None),
        P("tok"),
        P("tok"),
        P("tok", None),
        P("tok", None),
    )
    out_specs = P("tok", "head")
    return jax.shard_map(shards, mesh=mesh, in_specs=in_specs, out_specs=out_specs, check_vma=False)
```

```python
import jax
import jax.numpy as jnp
from jax import lax
from jax.sharding import PartitionSpec as P
from jax.experimental import pallas as pl
from jax.experimental.pallas import tpu as pltpu

HD = 128
ROT = 32


epsilon = 1e-05


def layer_norm(wide, gain, shift):
    row_mean = jnp.mean(wide, axis=1, keepdims=True)
    centred = wide - row_mean
    row_var = jnp.mean(centred * centred, axis=1, keepdims=True)
    return (centred * lax.rsqrt(row_var + epsilon) * gain + shift).astype(jnp.bfloat16)


def rotate(vectors, positions):
    half_rot = ROT // 2
    inv_freq = 10000.0 ** (-2.0 * jnp.arange(half_rot, dtype=jnp.float32) / ROT)
    angles = positions.astype(jnp.float32)[:, None] * inv_freq[None, :]
    cosine = jnp.cos(angles)[:, None, :]
    sine_part = jnp.sin(angles)[:, None, :]
    lower_half = vectors[..., :half_rot]
    upper_half = vectors[..., half_rot:ROT]
    return jnp.concatenate(
        [
            lower_half * cosine - upper_half * sine_part,
            upper_half * cosine + lower_half * sine_part,
            vectors[..., ROT:],
        ],
        axis=-1,
    )


def token_positions(local_req, cached):
    onehot = local_req[:, None] == jnp.arange(cached.shape[0], dtype=jnp.int32)[None, :]
    stretch_sizes = jnp.sum(onehot.astype(jnp.int32), axis=0)
    starts = jnp.cumsum(stretch_sizes) - stretch_sizes
    own_start = jnp.sum(jnp.where(onehot, starts[None, :], 0), axis=1)
    own_cached = jnp.sum(jnp.where(onehot, cached[None, :], 0), axis=1)
    return own_cached + jnp.arange(local_req.shape[0], dtype=jnp.int32) - own_start


def attend(queries, new_keys, new_values, cache_keys, cache_values, local_req, cached, positions):
    span = cache_keys.shape[0] // cached.shape[0]
    key_slot = jnp.arange(cache_keys.shape[0], dtype=jnp.int32)
    key_owner = key_slot // span
    key_place = key_slot % span
    cache_ok = (local_req[:, None] == key_owner[None, :]) & (
        key_place[None, :] < jnp.repeat(cached, span)[None, :]
    )
    new_ok = (local_req[:, None] == local_req[None, :]) & (positions[None, :] <= positions[:, None])
    allowed = jnp.concatenate([cache_ok, new_ok], axis=1)
    all_keys = jnp.concatenate([cache_keys, new_keys], axis=0)
    all_values = jnp.concatenate([cache_values, new_values], axis=0)
    scores = jnp.einsum(
        "thd,khd->htk", queries, all_keys, preferred_element_type=jnp.float32
    ) * HD ** (-0.5)
    scores = jnp.where(allowed[None], scores, -1e30)
    peak = jnp.max(scores, axis=2, keepdims=True)
    exp_scores = jnp.exp(scores - peak)
    attn_probs = (exp_scores / jnp.sum(exp_scores, axis=2, keepdims=True)).astype(jnp.bfloat16)
    return jnp.einsum(
        "htk,khd->thd", attn_probs, all_values, preferred_element_type=jnp.float32
    ).astype(jnp.bfloat16)


def attention_kernel(
    q_ref, kc_ref, vc_ref, kn_ref, vn_ref, req_col, pos_col, owner_row, limit_row, req_row, pos_row, o_ref
):
    queries = q_ref[...]
    cache_keys = kc_ref[...].reshape(-1, queries.shape[1])
    cache_values = vc_ref[...].reshape(-1, queries.shape[1])
    dims = (((1,), (1,)), ((), ()))
    scale = HD ** (-0.5)
    cache_scores = lax.dot_general(queries, cache_keys, dims, preferred_element_type=jnp.float32) * scale
    new_scores = lax.dot_general(queries, kn_ref[...], dims, preferred_element_type=jnp.float32) * scale
    cache_place = lax.broadcasted_iota(jnp.int32, cache_scores.shape, 1) % (
        cache_scores.shape[1] // 2
    )
    cache_ok = (req_col[...] == owner_row[...]) & (cache_place < limit_row[...])
    new_ok = (req_col[...] == req_row[...]) & (pos_row[...] <= pos_col[...])
    cache_scores = jnp.where(cache_ok, cache_scores, -1e30)
    new_scores = jnp.where(new_ok, new_scores, -1e30)
    peak = jnp.maximum(
        jnp.max(cache_scores, axis=1, keepdims=True), jnp.max(new_scores, axis=1, keepdims=True)
    )
    cache_exp = jnp.exp(cache_scores - peak)
    new_exp = jnp.exp(new_scores - peak)
    total = jnp.sum(cache_exp, axis=1, keepdims=True) + jnp.sum(new_exp, axis=1, keepdims=True)
    cache_probs = (cache_exp / total).astype(jnp.bfloat16)
    new_probs = (new_exp / total).astype(jnp.bfloat16)
    mixed = jnp.dot(cache_probs, cache_values, preferred_element_type=jnp.float32) + jnp.dot(
        new_probs, vn_ref[...], preferred_element_type=jnp.float32
    )
    o_ref[...] = mixed.astype(o_ref.dtype)


def attend_kernel(queries, new_keys, new_values, pages, local_req, cached, positions):
    tokens, heads = queries.shape[0], queries.shape[1]
    page_count, page_len = pages.shape[0], pages.shape[2]
    span = page_count * page_len // cached.shape[0]
    key_slot = jnp.arange(page_count * page_len, dtype=jnp.int32)
    owner_row = (key_slot // span)[None, :]
    limit_row = jnp.repeat(cached, span)[None, :]
    flat = lambda x: x.reshape(tokens, heads * HD)
    row_block = pl.BlockSpec((tokens, HD), lambda h: (0, h))
    page_block = lambda part: pl.BlockSpec((page_count, 1, page_len, HD), lambda h: (0, part, 0, h))
    whole = lambda x: pl.BlockSpec(x.shape, lambda h: (0,) * x.ndim)
    extras = (
        local_req[:, None],
        positions[:, None],
        owner_row,
        limit_row,
        local_req[None, :],
        positions[None, :],
    )
    keys_seen = page_count * page_len + tokens
    out = pl.pallas_call(
        attention_kernel,
        grid=(heads,),
        in_specs=[row_block, page_block(0), page_block(1), row_block, row_block]
        + [whole(x) for x in extras],
        out_specs=row_block,
        out_shape=jax.ShapeDtypeStruct((tokens, heads * HD), jnp.bfloat16),
        cost_estimate=pl.CostEstimate(
            flops=4 * heads * tokens * keys_seen * HD,
            transcendentals=heads * tokens * keys_seen,
            bytes_accessed=2 * HD * heads * (2 * tokens + 2 * keys_seen),
        ),
    )(flat(queries), pages, pages, flat(new_keys), flat(new_values), *extras)
    return out


def share_pages(local_pool, groups):
    grouped = local_pool.reshape(
        local_pool.shape[0], 2, local_pool.shape[2], groups, local_pool.shape[3] // groups
    )
    shared = lax.all_to_all(grouped, "head", split_axis=3, concat_axis=0, tiled=True)
    return shared.reshape(shared.shape[0], 2, shared.shape[2], shared.shape[4])


def gather_by_all_to_all(block, axis):
    count = lax.axis_size(axis)
    copies = jnp.broadcast_to(block[None], (count,) + block.shape).reshape(
        (count * block.shape[0],) + block.shape[1:]
    )
    return lax.all_to_all(copies, axis, split_axis=0, concat_axis=0, tiled=True)


def shards(
    states,
    pre_gain,
    pre_shift,
    mlp_gain,
    mlp_shift,
    qkv_weight,
    qkv_bias,
    out_weight,
    out_bias,
    up_weight,
    up_bias,
    down_weight,
    down_bias,
    kv_cache,
    token_request,
    cached_len,
    page_table,
    migrations,
):
    gathered = lax.all_gather(states, "head", axis=1, tiled=True)
    page_pool = share_pages(kv_cache, lax.axis_size("head"))
    qkv_weight, page_pool = lax.optimization_barrier((qkv_weight, page_pool))
    qkv_full = gather_by_all_to_all(qkv_weight, "tok")
    out_full = lax.all_gather(out_weight, "tok", axis=1, tiled=True)
    wide = gathered.astype(jnp.float32)
    pre_normed = layer_norm(wide, pre_gain, pre_shift)
    mlp_normed = layer_norm(wide, mlp_gain, mlp_shift)
    tok_rows = gathered.shape[0]

    def feed(normed):
        hidden = jax.nn.gelu(
            jnp.dot(normed, up_weight, preferred_element_type=jnp.float32) + up_bias,
            approximate=False,
        ).astype(jnp.bfloat16)
        return jnp.dot(hidden, down_weight, preferred_element_type=jnp.float32)

    feed_part = feed(mlp_normed)
    joined = jnp.dot(pre_normed, qkv_full, preferred_element_type=jnp.float32)
    joined = (joined + qkv_bias).reshape(tok_rows, -1, 3, HD)
    local_req = token_request - lax.axis_index("tok") * cached_len.shape[0]
    positions = token_positions(local_req, cached_len)
    queries = rotate(joined[:, :, 0], positions).astype(jnp.bfloat16)
    new_keys = rotate(joined[:, :, 1], positions).astype(jnp.bfloat16)
    new_values = joined[:, :, 2].astype(jnp.bfloat16)
    sources = migrations[:, 0]
    targets = migrations[:, 1]
    table = page_table.reshape(-1)
    match = table[:, None] == targets[None, :]
    moved_from = jnp.sum(jnp.where(match, sources[None, :], 0), axis=1)
    table = jnp.where(jnp.any(match, axis=1), moved_from, table)
    pages = page_pool[table]
    heads_out = attend_kernel(
        queries, new_keys, new_values, pages, local_req, cached_len, positions
    )
    attention_part = jnp.dot(heads_out, out_full, preferred_element_type=jnp.float32)
    summed = lax.psum_scatter(
        (attention_part + feed_part).astype(jnp.bfloat16), "head", scatter_dimension=1, tiled=True
    ).astype(jnp.float32)
    return (summed + out_bias + down_bias).astype(jnp.bfloat16)


def solution(mesh):
    in_specs = (
        P("tok", "head"),
        P(),
        P(),
        P(),
        P(),
        P("tok", "head"),
        P("head"),
        P("head", "tok"),
        P("head"),
        P(None, "head"),
        P("head"),
        P("head", None),
        P("head"),
        P(("tok", "head"), None, None, None),
        P("tok"),
        P("tok"),
        P("tok", None),
        P("tok", None),
    )
    out_specs = P("tok", "head")
    return jax.shard_map(shards, mesh=mesh, in_specs=in_specs, out_specs=out_specs, check_vma=False)
```

```python
import jax
import jax.numpy as jnp
from jax import lax
from jax.sharding import PartitionSpec as P
from jax.experimental import pallas as pl
from jax.experimental.pallas import tpu as pltpu

HD = 128
ROT = 32


epsilon = 1e-05


def layer_norm(wide, gain, shift):
    row_mean = jnp.mean(wide, axis=1, keepdims=True)
    centred = wide - row_mean
    row_var = jnp.mean(centred * centred, axis=1, keepdims=True)
    return (centred * lax.rsqrt(row_var + epsilon) * gain + shift).astype(jnp.bfloat16)


def rotate(vectors, positions):
    half_rot = ROT // 2
    inv_freq = 10000.0 ** (-2.0 * jnp.arange(half_rot, dtype=jnp.float32) / ROT)
    angles = positions.astype(jnp.float32)[:, None] * inv_freq[None, :]
    cosine = jnp.cos(angles)[:, None, :]
    sine_part = jnp.sin(angles)[:, None, :]
    lower_half = vectors[..., :half_rot]
    upper_half = vectors[..., half_rot:ROT]
    return jnp.concatenate(
        [
            lower_half * cosine - upper_half * sine_part,
            upper_half * cosine + lower_half * sine_part,
            vectors[..., ROT:],
        ],
        axis=-1,
    )


def token_positions(local_req, cached):
    onehot = local_req[:, None] == jnp.arange(cached.shape[0], dtype=jnp.int32)[None, :]
    stretch_sizes = jnp.sum(onehot.astype(jnp.int32), axis=0)
    starts = jnp.cumsum(stretch_sizes) - stretch_sizes
    own_start = jnp.sum(jnp.where(onehot, starts[None, :], 0), axis=1)
    own_cached = jnp.sum(jnp.where(onehot, cached[None, :], 0), axis=1)
    return own_cached + jnp.arange(local_req.shape[0], dtype=jnp.int32) - own_start


def attend(queries, new_keys, new_values, cache_keys, cache_values, local_req, cached, positions):
    span = cache_keys.shape[0] // cached.shape[0]
    key_slot = jnp.arange(cache_keys.shape[0], dtype=jnp.int32)
    key_owner = key_slot // span
    key_place = key_slot % span
    cache_ok = (local_req[:, None] == key_owner[None, :]) & (
        key_place[None, :] < jnp.repeat(cached, span)[None, :]
    )
    new_ok = (local_req[:, None] == local_req[None, :]) & (positions[None, :] <= positions[:, None])
    allowed = jnp.concatenate([cache_ok, new_ok], axis=1)
    all_keys = jnp.concatenate([cache_keys, new_keys], axis=0)
    all_values = jnp.concatenate([cache_values, new_values], axis=0)
    scores = jnp.einsum(
        "thd,khd->htk", queries, all_keys, preferred_element_type=jnp.float32
    ) * HD ** (-0.5)
    scores = jnp.where(allowed[None], scores, -1e30)
    peak = jnp.max(scores, axis=2, keepdims=True)
    exp_scores = jnp.exp(scores - peak)
    attn_probs = (exp_scores / jnp.sum(exp_scores, axis=2, keepdims=True)).astype(jnp.bfloat16)
    return jnp.einsum(
        "htk,khd->thd", attn_probs, all_values, preferred_element_type=jnp.float32
    ).astype(jnp.bfloat16)


def attention_kernel(q_ref, kc_ref, vc_ref, kn_ref, vn_ref, lo_col, hi_col, start_col, o_ref):
    queries = q_ref[...]
    cache_keys = kc_ref[...].reshape(-1, queries.shape[1])
    cache_values = vc_ref[...].reshape(-1, queries.shape[1])
    dims = (((1,), (1,)), ((), ()))
    scale = HD ** (-0.5)
    cache_scores = lax.dot_general(queries, cache_keys, dims, preferred_element_type=jnp.float32) * scale
    new_scores = lax.dot_general(queries, kn_ref[...], dims, preferred_element_type=jnp.float32) * scale
    cache_slot = lax.broadcasted_iota(jnp.int32, cache_scores.shape, 1)
    cache_ok = (cache_slot >= lo_col[...]) & (cache_slot < hi_col[...])
    new_slot = lax.broadcasted_iota(jnp.int32, new_scores.shape, 1)
    own_slot = lax.broadcasted_iota(jnp.int32, new_scores.shape, 0)
    new_ok = (new_slot >= start_col[...]) & (new_slot <= own_slot)
    cache_scores = jnp.where(cache_ok, cache_scores, -1e30)
    new_scores = jnp.where(new_ok, new_scores, -1e30)
    peak = jnp.maximum(
        jnp.max(cache_scores, axis=1, keepdims=True), jnp.max(new_scores, axis=1, keepdims=True)
    )
    cache_exp = jnp.exp(cache_scores - peak)
    new_exp = jnp.exp(new_scores - peak)
    total = jnp.sum(cache_exp, axis=1, keepdims=True) + jnp.sum(new_exp, axis=1, keepdims=True)
    cache_probs = (cache_exp / total).astype(jnp.bfloat16)
    new_probs = (new_exp / total).astype(jnp.bfloat16)
    mixed = jnp.dot(cache_probs, cache_values, preferred_element_type=jnp.float32) + jnp.dot(
        new_probs, vn_ref[...], preferred_element_type=jnp.float32
    )
    o_ref[...] = mixed.astype(o_ref.dtype)


def attend_kernel(queries, new_keys, new_values, pages, local_req, cached, positions):
    tokens, heads = queries.shape[0], queries.shape[1]
    page_count, page_len = pages.shape[0], pages.shape[2]
    span = page_count * page_len // cached.shape[0]
    own_cached = jnp.take(cached, local_req)
    lo_col = (local_req * span)[:, None]
    hi_col = lo_col + own_cached[:, None]
    start_col = (jnp.arange(tokens, dtype=jnp.int32) - positions + own_cached)[:, None]
    flat = lambda x: x.reshape(tokens, heads * HD)
    row_block = pl.BlockSpec((tokens, HD), lambda h: (0, h))
    page_block = lambda part: pl.BlockSpec((page_count, 1, page_len, HD), lambda h: (0, part, 0, h))
    whole = lambda x: pl.BlockSpec(x.shape, lambda h: (0,) * x.ndim)
    extras = (lo_col, hi_col, start_col)
    keys_seen = page_count * page_len + tokens
    out = pl.pallas_call(
        attention_kernel,
        grid=(heads,),
        in_specs=[row_block, page_block(0), page_block(1), row_block, row_block]
        + [whole(x) for x in extras],
        out_specs=row_block,
        out_shape=jax.ShapeDtypeStruct((tokens, heads * HD), jnp.bfloat16),
        cost_estimate=pl.CostEstimate(
            flops=4 * heads * tokens * keys_seen * HD,
            transcendentals=heads * tokens * keys_seen,
            bytes_accessed=2 * HD * heads * (2 * tokens + 2 * keys_seen),
        ),
    )(flat(queries), pages, pages, flat(new_keys), flat(new_values), *extras)
    return out


def share_pages(local_pool, groups):
    grouped = local_pool.reshape(
        local_pool.shape[0], 2, local_pool.shape[2], groups, local_pool.shape[3] // groups
    )
    shared = lax.all_to_all(grouped, "head", split_axis=3, concat_axis=0, tiled=True)
    return shared.reshape(shared.shape[0], 2, shared.shape[2], shared.shape[4])


def gather_by_all_to_all(block, axis):
    count = lax.axis_size(axis)
    copies = jnp.broadcast_to(block[None], (count,) + block.shape).reshape(
        (count * block.shape[0],) + block.shape[1:]
    )
    return lax.all_to_all(copies, axis, split_axis=0, concat_axis=0, tiled=True)


def shards(
    states,
    pre_gain,
    pre_shift,
    mlp_gain,
    mlp_shift,
    qkv_weight,
    qkv_bias,
    out_weight,
    out_bias,
    up_weight,
    up_bias,
    down_weight,
    down_bias,
    kv_cache,
    token_request,
    cached_len,
    page_table,
    migrations,
):
    gathered = lax.all_gather(states, "head", axis=1, tiled=True)
    qkv_full = gather_by_all_to_all(qkv_weight, "tok")
    out_full = lax.all_gather(out_weight, "tok", axis=1, tiled=True)
    wide = gathered.astype(jnp.float32)
    pre_normed = layer_norm(wide, pre_gain, pre_shift)
    mlp_normed = layer_norm(wide, mlp_gain, mlp_shift)
    tok_rows = gathered.shape[0]

    def feed(normed):
        hidden = jax.nn.gelu(
            jnp.dot(normed, up_weight, preferred_element_type=jnp.float32) + up_bias,
            approximate=False,
        ).astype(jnp.bfloat16)
        return jnp.dot(hidden, down_weight, preferred_element_type=jnp.float32)

    feed_part = feed(mlp_normed)
    kv_cache, feed_part = lax.optimization_barrier((kv_cache, feed_part))
    page_pool = share_pages(kv_cache, lax.axis_size("head"))
    joined = jnp.dot(pre_normed, qkv_full, preferred_element_type=jnp.float32)
    joined = (joined + qkv_bias).reshape(tok_rows, -1, 3, HD)
    local_req = token_request - lax.axis_index("tok") * cached_len.shape[0]
    positions = token_positions(local_req, cached_len)
    queries = rotate(joined[:, :, 0], positions).astype(jnp.bfloat16)
    new_keys = rotate(joined[:, :, 1], positions).astype(jnp.bfloat16)
    new_values = joined[:, :, 2].astype(jnp.bfloat16)
    sources = migrations[:, 0]
    targets = migrations[:, 1]
    table = page_table.reshape(-1)
    match = table[:, None] == targets[None, :]
    moved_from = jnp.sum(jnp.where(match, sources[None, :], 0), axis=1)
    table = jnp.where(jnp.any(match, axis=1), moved_from, table)
    pages = page_pool[table]
    heads_out = attend_kernel(
        queries, new_keys, new_values, pages, local_req, cached_len, positions
    )
    attention_part = jnp.dot(heads_out, out_full, preferred_element_type=jnp.float32)
    bias_row = lax.dynamic_update_slice_in_dim(
        jnp.zeros((attention_part.shape[1],), jnp.float32),
        out_bias + down_bias,
        lax.axis_index("head") * out_bias.shape[0],
        axis=0,
    )
    return lax.psum_scatter(
        (attention_part + feed_part + bias_row).astype(jnp.bfloat16),
        "head",
        scatter_dimension=1,
        tiled=True,
    )


def solution(mesh):
    in_specs = (
        P("tok", "head"),
        P(),
        P(),
        P(),
        P(),
        P("tok", "head"),
        P("head"),
        P("head", "tok"),
        P("head"),
        P(None, "head"),
        P("head"),
        P("head", None),
        P("head"),
        P(("tok", "head"), None, None, None),
        P("tok"),
        P("tok"),
        P("tok", None),
        P("tok", None),
    )
    out_specs = P("tok", "head")
    return jax.shard_map(shards, mesh=mesh, in_specs=in_specs, out_specs=out_specs, check_vma=False)
```

```python
import jax
import jax.numpy as jnp
from jax import lax
from jax.sharding import PartitionSpec as P
from jax.experimental import pallas as pl
from jax.experimental.pallas import tpu as pltpu

HD = 128
ROT = 32


epsilon = 1e-05


def layer_norm(wide, gain, shift):
    row_mean = jnp.mean(wide, axis=1, keepdims=True)
    centred = wide - row_mean
    row_var = jnp.mean(centred * centred, axis=1, keepdims=True)
    return (centred * lax.rsqrt(row_var + epsilon) * gain + shift).astype(jnp.bfloat16)


def rotate(vectors, positions):
    half_rot = ROT // 2
    inv_freq = 10000.0 ** (-2.0 * jnp.arange(half_rot, dtype=jnp.float32) / ROT)
    angles = positions.astype(jnp.float32)[:, None] * inv_freq[None, :]
    cosine = jnp.cos(angles)[:, None, :]
    sine_part = jnp.sin(angles)[:, None, :]
    lower_half = vectors[..., :half_rot]
    upper_half = vectors[..., half_rot:ROT]
    return jnp.concatenate(
        [
            lower_half * cosine - upper_half * sine_part,
            upper_half * cosine + lower_half * sine_part,
            vectors[..., ROT:],
        ],
        axis=-1,
    )


def token_positions(local_req, cached):
    onehot = local_req[:, None] == jnp.arange(cached.shape[0], dtype=jnp.int32)[None, :]
    stretch_sizes = jnp.sum(onehot.astype(jnp.int32), axis=0)
    starts = jnp.cumsum(stretch_sizes) - stretch_sizes
    own_start = jnp.sum(jnp.where(onehot, starts[None, :], 0), axis=1)
    own_cached = jnp.sum(jnp.where(onehot, cached[None, :], 0), axis=1)
    return own_cached + jnp.arange(local_req.shape[0], dtype=jnp.int32) - own_start


def attend(queries, new_keys, new_values, cache_keys, cache_values, local_req, cached, positions):
    span = cache_keys.shape[0] // cached.shape[0]
    key_slot = jnp.arange(cache_keys.shape[0], dtype=jnp.int32)
    key_owner = key_slot // span
    key_place = key_slot % span
    cache_ok = (local_req[:, None] == key_owner[None, :]) & (
        key_place[None, :] < jnp.repeat(cached, span)[None, :]
    )
    new_ok = (local_req[:, None] == local_req[None, :]) & (positions[None, :] <= positions[:, None])
    allowed = jnp.concatenate([cache_ok, new_ok], axis=1)
    all_keys = jnp.concatenate([cache_keys, new_keys], axis=0)
    all_values = jnp.concatenate([cache_values, new_values], axis=0)
    scores = jnp.einsum(
        "thd,khd->htk", queries, all_keys, preferred_element_type=jnp.float32
    ) * HD ** (-0.5)
    scores = jnp.where(allowed[None], scores, -1e30)
    peak = jnp.max(scores, axis=2, keepdims=True)
    exp_scores = jnp.exp(scores - peak)
    attn_probs = (exp_scores / jnp.sum(exp_scores, axis=2, keepdims=True)).astype(jnp.bfloat16)
    return jnp.einsum(
        "htk,khd->thd", attn_probs, all_values, preferred_element_type=jnp.float32
    ).astype(jnp.bfloat16)


def attention_kernel(q_ref, kc_ref, vc_ref, kn_ref, vn_ref, lo_col, hi_col, start_col, o_ref):
    queries = q_ref[...]
    cache_keys = kc_ref[...].reshape(-1, queries.shape[1])
    cache_values = vc_ref[...].reshape(-1, queries.shape[1])
    dims = (((1,), (1,)), ((), ()))
    scale = HD ** (-0.5)
    cache_scores = lax.dot_general(queries, cache_keys, dims, preferred_element_type=jnp.float32) * scale
    new_scores = lax.dot_general(queries, kn_ref[...], dims, preferred_element_type=jnp.float32) * scale
    cache_slot = lax.broadcasted_iota(jnp.int32, cache_scores.shape, 1)
    cache_ok = (cache_slot >= lo_col[...]) & (cache_slot < hi_col[...])
    new_slot = lax.broadcasted_iota(jnp.int32, new_scores.shape, 1)
    own_slot = lax.broadcasted_iota(jnp.int32, new_scores.shape, 0)
    new_ok = (new_slot >= start_col[...]) & (new_slot <= own_slot)
    cache_scores = jnp.where(cache_ok, cache_scores, -1e30)
    new_scores = jnp.where(new_ok, new_scores, -1e30)
    peak = jnp.maximum(
        jnp.max(cache_scores, axis=1, keepdims=True), jnp.max(new_scores, axis=1, keepdims=True)
    )
    cache_exp = jnp.exp(cache_scores - peak)
    new_exp = jnp.exp(new_scores - peak)
    total = jnp.sum(cache_exp, axis=1, keepdims=True) + jnp.sum(new_exp, axis=1, keepdims=True)
    inverse = 1.0 / total
    cache_probs = (cache_exp * inverse).astype(jnp.bfloat16)
    new_probs = (new_exp * inverse).astype(jnp.bfloat16)
    mixed = jnp.dot(cache_probs, cache_values, preferred_element_type=jnp.float32) + jnp.dot(
        new_probs, vn_ref[...], preferred_element_type=jnp.float32
    )
    o_ref[...] = mixed.astype(o_ref.dtype)


def attend_kernel(queries, new_keys, new_values, pages, local_req, cached, positions):
    tokens, heads = queries.shape[0], queries.shape[1]
    page_count, page_len = pages.shape[0], pages.shape[2]
    span = page_count * page_len // cached.shape[0]
    own_cached = jnp.take(cached, local_req)
    lo_col = (local_req * span)[:, None]
    hi_col = lo_col + own_cached[:, None]
    start_col = (jnp.arange(tokens, dtype=jnp.int32) - positions + own_cached)[:, None]
    flat = lambda x: x.reshape(tokens, heads * HD)
    row_block = pl.BlockSpec((tokens, HD), lambda h: (0, h))
    page_block = lambda part: pl.BlockSpec((page_count, 1, page_len, HD), lambda h: (0, part, 0, h))
    whole = lambda x: pl.BlockSpec(x.shape, lambda h: (0,) * x.ndim)
    extras = (lo_col, hi_col, start_col)
    keys_seen = page_count * page_len + tokens
    out = pl.pallas_call(
        attention_kernel,
        grid=(heads,),
        in_specs=[row_block, page_block(0), page_block(1), row_block, row_block]
        + [whole(x) for x in extras],
        out_specs=row_block,
        out_shape=jax.ShapeDtypeStruct((tokens, heads * HD), jnp.bfloat16),
        cost_estimate=pl.CostEstimate(
            flops=4 * heads * tokens * keys_seen * HD,
            transcendentals=heads * tokens * keys_seen,
            bytes_accessed=2 * HD * heads * (2 * tokens + 2 * keys_seen),
        ),
    )(flat(queries), pages, pages, flat(new_keys), flat(new_values), *extras)
    return out


def project_kernel(heads_ref, weight_ref, feed_ref, bias_ref, o_ref):
    product = jnp.dot(heads_ref[...], weight_ref[...], preferred_element_type=jnp.float32)
    o_ref[...] = (product + feed_ref[...] + bias_ref[...]).astype(o_ref.dtype)


def project_and_add(heads_out, weight, feed_part, bias_row):
    tokens, width = feed_part.shape
    tile = 512
    return pl.pallas_call(
        project_kernel,
        grid=(width // tile,),
        in_specs=[
            pl.BlockSpec(heads_out.shape, lambda j: (0, 0)),
            pl.BlockSpec((weight.shape[0], tile), lambda j: (0, j)),
            pl.BlockSpec((tokens, tile), lambda j: (0, j)),
            pl.BlockSpec((1, tile), lambda j: (0, j)),
        ],
        out_specs=pl.BlockSpec((tokens, tile), lambda j: (0, j)),
        out_shape=jax.ShapeDtypeStruct((tokens, width), jnp.bfloat16),
        cost_estimate=pl.CostEstimate(
            flops=2 * tokens * heads_out.shape[1] * width,
            transcendentals=0,
            bytes_accessed=2 * heads_out.size + 2 * weight.size + 4 * feed_part.size + 2 * tokens * width,
        ),
    )(heads_out, weight, feed_part, bias_row[None, :])


def share_pages(local_pool, groups):
    grouped = local_pool.reshape(
        local_pool.shape[0], 2, local_pool.shape[2], groups, local_pool.shape[3] // groups
    )
    shared = lax.all_to_all(grouped, "head", split_axis=3, concat_axis=0, tiled=True)
    return shared.reshape(shared.shape[0], 2, shared.shape[2], shared.shape[4])


def gather_by_all_to_all(block, axis):
    count = lax.axis_size(axis)
    copies = jnp.broadcast_to(block[None], (count,) + block.shape).reshape(
        (count * block.shape[0],) + block.shape[1:]
    )
    return lax.all_to_all(copies, axis, split_axis=0, concat_axis=0, tiled=True)


def shards(
    states,
    pre_gain,
    pre_shift,
    mlp_gain,
    mlp_shift,
    qkv_weight,
    qkv_bias,
    out_weight,
    out_bias,
    up_weight,
    up_bias,
    down_weight,
    down_bias,
    kv_cache,
    token_request,
    cached_len,
    page_table,
    migrations,
):
    gathered = lax.all_gather(states, "head", axis=1, tiled=True)
    qkv_full = gather_by_all_to_all(qkv_weight, "tok")
    out_full = lax.all_gather(out_weight, "tok", axis=1, tiled=True)
    wide = gathered.astype(jnp.float32)
    pre_normed = layer_norm(wide, pre_gain, pre_shift)
    mlp_normed = layer_norm(wide, mlp_gain, mlp_shift)
    tok_rows = gathered.shape[0]

    def feed(normed):
        hidden = jax.nn.gelu(
            jnp.dot(normed, up_weight, preferred_element_type=jnp.float32) + up_bias,
            approximate=False,
        ).astype(jnp.bfloat16)
        return jnp.dot(hidden, down_weight, preferred_element_type=jnp.float32)

    feed_part = feed(mlp_normed)
    kv_cache, feed_part = lax.optimization_barrier((kv_cache, feed_part))
    page_pool = share_pages(kv_cache, lax.axis_size("head"))
    joined = jnp.dot(pre_normed, qkv_full, preferred_element_type=jnp.float32)
    joined = (joined + qkv_bias).reshape(tok_rows, -1, 3, HD)
    local_req = token_request - lax.axis_index("tok") * cached_len.shape[0]
    positions = token_positions(local_req, cached_len)
    queries = rotate(joined[:, :, 0], positions).astype(jnp.bfloat16)
    new_keys = rotate(joined[:, :, 1], positions).astype(jnp.bfloat16)
    new_values = joined[:, :, 2].astype(jnp.bfloat16)
    sources = migrations[:, 0]
    targets = migrations[:, 1]
    table = page_table.reshape(-1)
    match = table[:, None] == targets[None, :]
    moved_from = jnp.sum(jnp.where(match, sources[None, :], 0), axis=1)
    table = jnp.where(jnp.any(match, axis=1), moved_from, table)
    pages = page_pool[table]
    heads_out = attend_kernel(
        queries, new_keys, new_values, pages, local_req, cached_len, positions
    )
    bias_row = lax.dynamic_update_slice_in_dim(
        jnp.zeros((out_full.shape[1],), jnp.float32),
        out_bias + down_bias,
        lax.axis_index("head") * out_bias.shape[0],
        axis=0,
    )
    return lax.psum_scatter(
        project_and_add(heads_out, out_full, feed_part, bias_row),
        "head",
        scatter_dimension=1,
        tiled=True,
    )


def solution(mesh):
    in_specs = (
        P("tok", "head"),
        P(),
        P(),
        P(),
        P(),
        P("tok", "head"),
        P("head"),
        P("head", "tok"),
        P("head"),
        P(None, "head"),
        P("head"),
        P("head", None),
        P("head"),
        P(("tok", "head"), None, None, None),
        P("tok"),
        P("tok"),
        P("tok", None),
        P("tok", None),
    )
    out_specs = P("tok", "head")
    return jax.shard_map(shards, mesh=mesh, in_specs=in_specs, out_specs=out_specs, check_vma=False)
```

```python
import jax
import jax.numpy as jnp
from jax import lax
from jax.sharding import PartitionSpec as P
from jax.experimental import pallas as pl
from jax.experimental.pallas import tpu as pltpu

HD = 128
ROT = 32


epsilon = 1e-05


def layer_norm(wide, gain, shift):
    row_mean = jnp.mean(wide, axis=1, keepdims=True)
    centred = wide - row_mean
    row_var = jnp.mean(centred * centred, axis=1, keepdims=True)
    return (centred * lax.rsqrt(row_var + epsilon) * gain + shift).astype(jnp.bfloat16)


def rotate(vectors, positions):
    half_rot = ROT // 2
    inv_freq = 10000.0 ** (-2.0 * jnp.arange(half_rot, dtype=jnp.float32) / ROT)
    angles = positions.astype(jnp.float32)[:, None] * inv_freq[None, :]
    cosine = jnp.cos(angles)[:, None, :]
    sine_part = jnp.sin(angles)[:, None, :]
    lower_half = vectors[..., :half_rot]
    upper_half = vectors[..., half_rot:ROT]
    return jnp.concatenate(
        [
            lower_half * cosine - upper_half * sine_part,
            upper_half * cosine + lower_half * sine_part,
            vectors[..., ROT:],
        ],
        axis=-1,
    )


def token_positions(local_req, cached):
    onehot = local_req[:, None] == jnp.arange(cached.shape[0], dtype=jnp.int32)[None, :]
    stretch_sizes = jnp.sum(onehot.astype(jnp.int32), axis=0)
    starts = jnp.cumsum(stretch_sizes) - stretch_sizes
    own_start = jnp.sum(jnp.where(onehot, starts[None, :], 0), axis=1)
    own_cached = jnp.sum(jnp.where(onehot, cached[None, :], 0), axis=1)
    return own_cached + jnp.arange(local_req.shape[0], dtype=jnp.int32) - own_start


def attend(queries, new_keys, new_values, cache_keys, cache_values, local_req, cached, positions):
    span = cache_keys.shape[0] // cached.shape[0]
    key_slot = jnp.arange(cache_keys.shape[0], dtype=jnp.int32)
    key_owner = key_slot // span
    key_place = key_slot % span
    cache_ok = (local_req[:, None] == key_owner[None, :]) & (
        key_place[None, :] < jnp.repeat(cached, span)[None, :]
    )
    new_ok = (local_req[:, None] == local_req[None, :]) & (positions[None, :] <= positions[:, None])
    allowed = jnp.concatenate([cache_ok, new_ok], axis=1)
    all_keys = jnp.concatenate([cache_keys, new_keys], axis=0)
    all_values = jnp.concatenate([cache_values, new_values], axis=0)
    scores = jnp.einsum(
        "thd,khd->htk", queries, all_keys, preferred_element_type=jnp.float32
    ) * HD ** (-0.5)
    scores = jnp.where(allowed[None], scores, -1e30)
    peak = jnp.max(scores, axis=2, keepdims=True)
    exp_scores = jnp.exp(scores - peak)
    attn_probs = (exp_scores / jnp.sum(exp_scores, axis=2, keepdims=True)).astype(jnp.bfloat16)
    return jnp.einsum(
        "htk,khd->thd", attn_probs, all_values, preferred_element_type=jnp.float32
    ).astype(jnp.bfloat16)


def attention_kernel(q_ref, kc_ref, vc_ref, kn_ref, vn_ref, lo_col, hi_col, start_col, o_ref):
    queries = q_ref[...]
    cache_keys = kc_ref[...].reshape(-1, queries.shape[1])
    cache_values = vc_ref[...].reshape(-1, queries.shape[1])
    dims = (((1,), (1,)), ((), ()))
    scale = HD ** (-0.5)
    cache_scores = lax.dot_general(queries, cache_keys, dims, preferred_element_type=jnp.float32) * scale
    new_scores = lax.dot_general(queries, kn_ref[...], dims, preferred_element_type=jnp.float32) * scale
    cache_slot = lax.broadcasted_iota(jnp.int32, cache_scores.shape, 1)
    cache_ok = (cache_slot >= lo_col[...]) & (cache_slot < hi_col[...])
    new_slot = lax.broadcasted_iota(jnp.int32, new_scores.shape, 1)
    own_slot = lax.broadcasted_iota(jnp.int32, new_scores.shape, 0)
    new_ok = (new_slot >= start_col[...]) & (new_slot <= own_slot)
    cache_scores = jnp.where(cache_ok, cache_scores, -1e30)
    new_scores = jnp.where(new_ok, new_scores, -1e30)
    peak = jnp.maximum(
        jnp.max(cache_scores, axis=1, keepdims=True), jnp.max(new_scores, axis=1, keepdims=True)
    )
    cache_exp = jnp.exp(cache_scores - peak)
    new_exp = jnp.exp(new_scores - peak)
    total = jnp.sum(cache_exp, axis=1, keepdims=True) + jnp.sum(new_exp, axis=1, keepdims=True)
    cache_probs = (cache_exp / total).astype(jnp.bfloat16)
    new_probs = (new_exp / total).astype(jnp.bfloat16)
    mixed = jnp.dot(cache_probs, cache_values, preferred_element_type=jnp.float32) + jnp.dot(
        new_probs, vn_ref[...], preferred_element_type=jnp.float32
    )
    o_ref[...] = mixed.astype(o_ref.dtype)


def attend_kernel(queries, new_keys, new_values, pages, local_req, cached, positions):
    tokens, heads = queries.shape[0], queries.shape[1]
    page_count, page_len = pages.shape[0], pages.shape[2]
    span = page_count * page_len // cached.shape[0]
    own_cached = jnp.take(cached, local_req)
    lo_col = (local_req * span)[:, None]
    hi_col = lo_col + own_cached[:, None]
    start_col = (jnp.arange(tokens, dtype=jnp.int32) - positions + own_cached)[:, None]
    flat = lambda x: x.reshape(tokens, heads * HD)
    row_block = pl.BlockSpec((tokens, HD), lambda h: (0, h))
    page_block = lambda part: pl.BlockSpec((page_count, 1, page_len, HD), lambda h: (0, part, 0, h))
    whole = lambda x: pl.BlockSpec(x.shape, lambda h: (0,) * x.ndim)
    extras = (lo_col, hi_col, start_col)
    keys_seen = page_count * page_len + tokens
    out = pl.pallas_call(
        attention_kernel,
        grid=(heads,),
        in_specs=[row_block, page_block(0), page_block(1), row_block, row_block]
        + [whole(x) for x in extras],
        out_specs=row_block,
        out_shape=jax.ShapeDtypeStruct((tokens, heads * HD), jnp.bfloat16),
        cost_estimate=pl.CostEstimate(
            flops=4 * heads * tokens * keys_seen * HD,
            transcendentals=heads * tokens * keys_seen,
            bytes_accessed=2 * HD * heads * (2 * tokens + 2 * keys_seen),
        ),
    )(flat(queries), pages, pages, flat(new_keys), flat(new_values), *extras)
    return out


def share_pages(local_pool, groups):
    grouped = local_pool.reshape(
        local_pool.shape[0], 2, local_pool.shape[2], groups, local_pool.shape[3] // groups
    )
    shared = lax.all_to_all(grouped, "head", split_axis=3, concat_axis=0, tiled=True)
    return shared.reshape(shared.shape[0], 2, shared.shape[2], shared.shape[4])


def gather_by_all_to_all(block, axis):
    count = lax.axis_size(axis)
    copies = jnp.broadcast_to(block[None], (count,) + block.shape).reshape(
        (count * block.shape[0],) + block.shape[1:]
    )
    return lax.all_to_all(copies, axis, split_axis=0, concat_axis=0, tiled=True)


def shards(
    states,
    pre_gain,
    pre_shift,
    mlp_gain,
    mlp_shift,
    qkv_weight,
    qkv_bias,
    out_weight,
    out_bias,
    up_weight,
    up_bias,
    down_weight,
    down_bias,
    kv_cache,
    token_request,
    cached_len,
    page_table,
    migrations,
):
    gathered = lax.all_gather(states, "head", axis=1, tiled=True)
    qkv_full = gather_by_all_to_all(qkv_weight, "tok")
    out_full = lax.all_gather(out_weight, "tok", axis=1, tiled=True)
    wide = gathered.astype(jnp.float32)
    pre_normed = layer_norm(wide, pre_gain, pre_shift)
    mlp_normed = layer_norm(wide, mlp_gain, mlp_shift)
    tok_rows = gathered.shape[0]

    def feed(normed):
        hidden = jax.nn.gelu(
            jnp.dot(normed, up_weight, preferred_element_type=jnp.float32) + up_bias,
            approximate=False,
        ).astype(jnp.bfloat16)
        return jnp.dot(hidden, down_weight, preferred_element_type=jnp.float32).astype(jnp.bfloat16)

    feed_part = feed(mlp_normed)
    kv_cache, feed_part = lax.optimization_barrier((kv_cache, feed_part))
    page_pool = share_pages(kv_cache, lax.axis_size("head"))
    joined = jnp.dot(pre_normed, qkv_full, preferred_element_type=jnp.float32)
    joined = (joined + qkv_bias).reshape(tok_rows, -1, 3, HD)
    local_req = token_request - lax.axis_index("tok") * cached_len.shape[0]
    positions = token_positions(local_req, cached_len)
    queries = rotate(joined[:, :, 0], positions).astype(jnp.bfloat16)
    new_keys = rotate(joined[:, :, 1], positions).astype(jnp.bfloat16)
    new_values = joined[:, :, 2].astype(jnp.bfloat16)
    sources = migrations[:, 0]
    targets = migrations[:, 1]
    table = page_table.reshape(-1)
    match = table[:, None] == targets[None, :]
    moved_from = jnp.sum(jnp.where(match, sources[None, :], 0), axis=1)
    table = jnp.where(jnp.any(match, axis=1), moved_from, table)
    pages = page_pool[table]
    heads_out = attend_kernel(
        queries, new_keys, new_values, pages, local_req, cached_len, positions
    )
    attention_part = jnp.dot(heads_out, out_full, preferred_element_type=jnp.float32)
    bias_row = lax.dynamic_update_slice_in_dim(
        jnp.zeros((attention_part.shape[1],), jnp.float32),
        out_bias + down_bias,
        lax.axis_index("head") * out_bias.shape[0],
        axis=0,
    )
    return lax.psum_scatter(
        (attention_part + feed_part + bias_row).astype(jnp.bfloat16),
        "head",
        scatter_dimension=1,
        tiled=True,
    )


def solution(mesh):
    in_specs = (
        P("tok", "head"),
        P(),
        P(),
        P(),
        P(),
        P("tok", "head"),
        P("head"),
        P("head", "tok"),
        P("head"),
        P(None, "head"),
        P("head"),
        P("head", None),
        P("head"),
        P(("tok", "head"), None, None, None),
        P("tok"),
        P("tok"),
        P("tok", None),
        P("tok", None),
    )
    out_specs = P("tok", "head")
    return jax.shard_map(shards, mesh=mesh, in_specs=in_specs, out_specs=out_specs, check_vma=False)
```

```python
import jax
import jax.numpy as jnp
from jax import lax
from jax.sharding import PartitionSpec as P
from jax.experimental import pallas as pl
from jax.experimental.pallas import tpu as pltpu

HD = 128
ROT = 32


epsilon = 1e-05


def layer_norm(wide, gain, shift):
    row_mean = jnp.mean(wide, axis=1, keepdims=True)
    centred = wide - row_mean
    row_var = jnp.mean(centred * centred, axis=1, keepdims=True)
    return (centred * lax.rsqrt(row_var + epsilon) * gain + shift).astype(jnp.bfloat16)


def rotate(vectors, positions):
    half_rot = ROT // 2
    inv_freq = 10000.0 ** (-2.0 * jnp.arange(half_rot, dtype=jnp.float32) / ROT)
    angles = positions.astype(jnp.float32)[:, None] * inv_freq[None, :]
    cosine = jnp.cos(angles)[:, None, :]
    sine_part = jnp.sin(angles)[:, None, :]
    lower_half = vectors[..., :half_rot]
    upper_half = vectors[..., half_rot:ROT]
    return jnp.concatenate(
        [
            lower_half * cosine - upper_half * sine_part,
            upper_half * cosine + lower_half * sine_part,
            vectors[..., ROT:],
        ],
        axis=-1,
    )


def token_positions(local_req, cached):
    onehot = local_req[:, None] == jnp.arange(cached.shape[0], dtype=jnp.int32)[None, :]
    stretch_sizes = jnp.sum(onehot.astype(jnp.int32), axis=0)
    starts = jnp.cumsum(stretch_sizes) - stretch_sizes
    own_start = jnp.sum(jnp.where(onehot, starts[None, :], 0), axis=1)
    own_cached = jnp.sum(jnp.where(onehot, cached[None, :], 0), axis=1)
    return own_cached + jnp.arange(local_req.shape[0], dtype=jnp.int32) - own_start


def attend(queries, new_keys, new_values, cache_keys, cache_values, local_req, cached, positions):
    span = cache_keys.shape[0] // cached.shape[0]
    key_slot = jnp.arange(cache_keys.shape[0], dtype=jnp.int32)
    key_owner = key_slot // span
    key_place = key_slot % span
    cache_ok = (local_req[:, None] == key_owner[None, :]) & (
        key_place[None, :] < jnp.repeat(cached, span)[None, :]
    )
    new_ok = (local_req[:, None] == local_req[None, :]) & (positions[None, :] <= positions[:, None])
    allowed = jnp.concatenate([cache_ok, new_ok], axis=1)
    all_keys = jnp.concatenate([cache_keys, new_keys], axis=0)
    all_values = jnp.concatenate([cache_values, new_values], axis=0)
    scores = jnp.einsum(
        "thd,khd->htk", queries, all_keys, preferred_element_type=jnp.float32
    ) * HD ** (-0.5)
    scores = jnp.where(allowed[None], scores, -1e30)
    peak = jnp.max(scores, axis=2, keepdims=True)
    exp_scores = jnp.exp(scores - peak)
    attn_probs = (exp_scores / jnp.sum(exp_scores, axis=2, keepdims=True)).astype(jnp.bfloat16)
    return jnp.einsum(
        "htk,khd->thd", attn_probs, all_values, preferred_element_type=jnp.float32
    ).astype(jnp.bfloat16)


def scores_kernel(q_ref, kc_ref, kn_ref, vn_ref, lo_col, hi_col, start_col, p_ref, n_ref):
    queries = q_ref[...]
    cache_keys = kc_ref[...].reshape(-1, queries.shape[1])
    dims = (((1,), (1,)), ((), ()))
    scale = HD ** (-0.5)
    cache_scores = lax.dot_general(queries, cache_keys, dims, preferred_element_type=jnp.float32) * scale
    new_scores = lax.dot_general(queries, kn_ref[...], dims, preferred_element_type=jnp.float32) * scale
    cache_slot = lax.broadcasted_iota(jnp.int32, cache_scores.shape, 1)
    cache_ok = (cache_slot >= lo_col[...]) & (cache_slot < hi_col[...])
    new_slot = lax.broadcasted_iota(jnp.int32, new_scores.shape, 1)
    own_slot = lax.broadcasted_iota(jnp.int32, new_scores.shape, 0)
    new_ok = (new_slot >= start_col[...]) & (new_slot <= own_slot)
    cache_scores = jnp.where(cache_ok, cache_scores, -1e30)
    new_scores = jnp.where(new_ok, new_scores, -1e30)
    peak = jnp.maximum(
        jnp.max(cache_scores, axis=1, keepdims=True), jnp.max(new_scores, axis=1, keepdims=True)
    )
    cache_exp = jnp.exp(cache_scores - peak)
    new_exp = jnp.exp(new_scores - peak)
    total = jnp.sum(cache_exp, axis=1, keepdims=True) + jnp.sum(new_exp, axis=1, keepdims=True)
    p_ref[0] = (cache_exp / total).astype(jnp.bfloat16)
    new_probs = (new_exp / total).astype(jnp.bfloat16)
    n_ref[...] = jnp.dot(new_probs, vn_ref[...], preferred_element_type=jnp.float32)


def values_kernel(p_ref, vc_ref, n_ref, o_ref):
    cache_values = vc_ref[...].reshape(-1, o_ref.shape[1])
    mixed = jnp.dot(p_ref[0], cache_values, preferred_element_type=jnp.float32) + n_ref[...]
    o_ref[...] = mixed.astype(o_ref.dtype)


def attend_kernel(queries, new_keys, new_values, key_pages, value_pool, table, local_req, cached, positions):
    tokens, heads = queries.shape[0], queries.shape[1]
    page_count, page_len = key_pages.shape[0], key_pages.shape[2]
    keys_cached = page_count * page_len
    span = keys_cached // cached.shape[0]
    own_cached = jnp.take(cached, local_req)
    lo_col = (local_req * span)[:, None]
    hi_col = lo_col + own_cached[:, None]
    start_col = (jnp.arange(tokens, dtype=jnp.int32) - positions + own_cached)[:, None]
    flat = lambda x: x.reshape(tokens, heads * HD)
    row_block = pl.BlockSpec((tokens, HD), lambda h: (0, h))
    page_block = pl.BlockSpec((page_count, 1, page_len, HD), lambda h: (0, 0, 0, h))
    prob_block = pl.BlockSpec((1, tokens, keys_cached), lambda h: (h, 0, 0))
    whole = lambda x: pl.BlockSpec(x.shape, lambda h: (0,) * x.ndim)
    extras = (lo_col, hi_col, start_col)
    keys_seen = keys_cached + tokens
    probs, partial = pl.pallas_call(
        scores_kernel,
        grid=(heads,),
        in_specs=[row_block, page_block, row_block, row_block] + [whole(x) for x in extras],
        out_specs=[prob_block, row_block],
        out_shape=[
            jax.ShapeDtypeStruct((heads, tokens, keys_cached), jnp.bfloat16),
            jax.ShapeDtypeStruct((tokens, heads * HD), jnp.float32),
        ],
        cost_estimate=pl.CostEstimate(
            flops=2 * heads * tokens * (keys_seen + tokens) * HD,
            transcendentals=heads * tokens * keys_seen,
            bytes_accessed=2 * HD * heads * (3 * tokens + keys_cached) + 2 * heads * tokens * keys_cached,
        ),
    )(flat(queries), key_pages, flat(new_keys), flat(new_values), *extras)
    value_pool, probs = lax.optimization_barrier((value_pool, probs))
    value_pages = value_pool[table]
    return pl.pallas_call(
        values_kernel,
        grid=(heads,),
        in_specs=[prob_block, page_block, row_block],
        out_specs=row_block,
        out_shape=jax.ShapeDtypeStruct((tokens, heads * HD), jnp.bfloat16),
        cost_estimate=pl.CostEstimate(
            flops=2 * heads * tokens * keys_cached * HD,
            transcendentals=0,
            bytes_accessed=2 * heads * tokens * keys_cached + 2 * HD * heads * keys_cached + 6 * tokens * heads * HD,
        ),
    )(probs, value_pages, partial)


def share_pages(local_pool, groups):
    grouped = local_pool.reshape(local_pool.shape[:3] + (groups, local_pool.shape[3] // groups))
    shared = lax.all_to_all(grouped, "head", split_axis=3, concat_axis=0, tiled=True)
    return shared.reshape(shared.shape[:3] + (shared.shape[4],))


def gather_by_all_to_all(block, axis):
    count = lax.axis_size(axis)
    copies = jnp.broadcast_to(block[None], (count,) + block.shape).reshape(
        (count * block.shape[0],) + block.shape[1:]
    )
    return lax.all_to_all(copies, axis, split_axis=0, concat_axis=0, tiled=True)


def shards(
    states,
    pre_gain,
    pre_shift,
    mlp_gain,
    mlp_shift,
    qkv_weight,
    qkv_bias,
    out_weight,
    out_bias,
    up_weight,
    up_bias,
    down_weight,
    down_bias,
    kv_cache,
    token_request,
    cached_len,
    page_table,
    migrations,
):
    gathered = lax.all_gather(states, "head", axis=1, tiled=True)
    qkv_full = gather_by_all_to_all(qkv_weight, "tok")
    out_full = lax.all_gather(out_weight, "tok", axis=1, tiled=True)
    wide = gathered.astype(jnp.float32)
    pre_normed = layer_norm(wide, pre_gain, pre_shift)
    mlp_normed = layer_norm(wide, mlp_gain, mlp_shift)
    tok_rows = gathered.shape[0]

    def feed(normed):
        hidden = jax.nn.gelu(
            jnp.dot(normed, up_weight, preferred_element_type=jnp.float32) + up_bias,
            approximate=False,
        ).astype(jnp.bfloat16)
        return jnp.dot(hidden, down_weight, preferred_element_type=jnp.float32).astype(jnp.bfloat16)

    feed_part = feed(mlp_normed)
    kv_cache, feed_part = lax.optimization_barrier((kv_cache, feed_part))
    key_pool = share_pages(kv_cache[:, :1], lax.axis_size("head"))
    value_pool = share_pages(kv_cache[:, 1:], lax.axis_size("head"))
    joined = jnp.dot(pre_normed, qkv_full, preferred_element_type=jnp.float32)
    joined = (joined + qkv_bias).reshape(tok_rows, -1, 3, HD)
    local_req = token_request - lax.axis_index("tok") * cached_len.shape[0]
    positions = token_positions(local_req, cached_len)
    queries = rotate(joined[:, :, 0], positions).astype(jnp.bfloat16)
    new_keys = rotate(joined[:, :, 1], positions).astype(jnp.bfloat16)
    new_values = joined[:, :, 2].astype(jnp.bfloat16)
    sources = migrations[:, 0]
    targets = migrations[:, 1]
    table = page_table.reshape(-1)
    match = table[:, None] == targets[None, :]
    moved_from = jnp.sum(jnp.where(match, sources[None, :], 0), axis=1)
    table = jnp.where(jnp.any(match, axis=1), moved_from, table)
    heads_out = attend_kernel(
        queries, new_keys, new_values, key_pool[table], value_pool, table, local_req, cached_len, positions
    )
    attention_part = jnp.dot(heads_out, out_full, preferred_element_type=jnp.float32)
    bias_row = lax.dynamic_update_slice_in_dim(
        jnp.zeros((attention_part.shape[1],), jnp.float32),
        out_bias + down_bias,
        lax.axis_index("head") * out_bias.shape[0],
        axis=0,
    )
    return lax.psum_scatter(
        (attention_part + feed_part + bias_row).astype(jnp.bfloat16),
        "head",
        scatter_dimension=1,
        tiled=True,
    )


def solution(mesh):
    in_specs = (
        P("tok", "head"),
        P(),
        P(),
        P(),
        P(),
        P("tok", "head"),
        P("head"),
        P("head", "tok"),
        P("head"),
        P(None, "head"),
        P("head"),
        P("head", None),
        P("head"),
        P(("tok", "head"), None, None, None),
        P("tok"),
        P("tok"),
        P("tok", None),
        P("tok", None),
    )
    out_specs = P("tok", "head")
    return jax.shard_map(shards, mesh=mesh, in_specs=in_specs, out_specs=out_specs, check_vma=False)
```

```python
import jax
import jax.numpy as jnp
from jax import lax
from jax.sharding import PartitionSpec as P
from jax.experimental import pallas as pl
from jax.experimental.pallas import tpu as pltpu

HD = 128
ROT = 32


epsilon = 1e-05


def layer_norm(wide, gain, shift):
    row_mean = jnp.mean(wide, axis=1, keepdims=True)
    centred = wide - row_mean
    row_var = jnp.mean(centred * centred, axis=1, keepdims=True)
    return (centred * lax.rsqrt(row_var + epsilon) * gain + shift).astype(jnp.bfloat16)


def rotate(vectors, positions):
    half_rot = ROT // 2
    inv_freq = 10000.0 ** (-2.0 * jnp.arange(half_rot, dtype=jnp.float32) / ROT)
    angles = positions.astype(jnp.float32)[:, None] * inv_freq[None, :]
    cosine = jnp.cos(angles)[:, None, :]
    sine_part = jnp.sin(angles)[:, None, :]
    lower_half = vectors[..., :half_rot]
    upper_half = vectors[..., half_rot:ROT]
    return jnp.concatenate(
        [
            lower_half * cosine - upper_half * sine_part,
            upper_half * cosine + lower_half * sine_part,
            vectors[..., ROT:],
        ],
        axis=-1,
    )


def token_positions(local_req, cached):
    onehot = local_req[:, None] == jnp.arange(cached.shape[0], dtype=jnp.int32)[None, :]
    stretch_sizes = jnp.sum(onehot.astype(jnp.int32), axis=0)
    starts = jnp.cumsum(stretch_sizes) - stretch_sizes
    own_start = jnp.sum(jnp.where(onehot, starts[None, :], 0), axis=1)
    own_cached = jnp.sum(jnp.where(onehot, cached[None, :], 0), axis=1)
    return own_cached + jnp.arange(local_req.shape[0], dtype=jnp.int32) - own_start


def attend(queries, new_keys, new_values, cache_keys, cache_values, local_req, cached, positions):
    span = cache_keys.shape[0] // cached.shape[0]
    key_slot = jnp.arange(cache_keys.shape[0], dtype=jnp.int32)
    key_owner = key_slot // span
    key_place = key_slot % span
    cache_ok = (local_req[:, None] == key_owner[None, :]) & (
        key_place[None, :] < jnp.repeat(cached, span)[None, :]
    )
    new_ok = (local_req[:, None] == local_req[None, :]) & (positions[None, :] <= positions[:, None])
    allowed = jnp.concatenate([cache_ok, new_ok], axis=1)
    all_keys = jnp.concatenate([cache_keys, new_keys], axis=0)
    all_values = jnp.concatenate([cache_values, new_values], axis=0)
    scores = jnp.einsum(
        "thd,khd->htk", queries, all_keys, preferred_element_type=jnp.float32
    ) * HD ** (-0.5)
    scores = jnp.where(allowed[None], scores, -1e30)
    peak = jnp.max(scores, axis=2, keepdims=True)
    exp_scores = jnp.exp(scores - peak)
    attn_probs = (exp_scores / jnp.sum(exp_scores, axis=2, keepdims=True)).astype(jnp.bfloat16)
    return jnp.einsum(
        "htk,khd->thd", attn_probs, all_values, preferred_element_type=jnp.float32
    ).astype(jnp.bfloat16)


def attention_kernel(q_ref, kc_ref, vc_ref, kn_ref, vn_ref, lo_col, hi_col, start_col, o_ref):
    queries = q_ref[...]
    cache_keys = kc_ref[...].reshape(-1, queries.shape[1])
    cache_values = vc_ref[...].reshape(-1, queries.shape[1])
    dims = (((1,), (1,)), ((), ()))
    scale = HD ** (-0.5)
    cache_scores = lax.dot_general(queries, cache_keys, dims, preferred_element_type=jnp.float32) * scale
    new_scores = lax.dot_general(queries, kn_ref[...], dims, preferred_element_type=jnp.float32) * scale
    cache_slot = lax.broadcasted_iota(jnp.int32, cache_scores.shape, 1)
    cache_ok = (cache_slot >= lo_col[...]) & (cache_slot < hi_col[...])
    new_slot = lax.broadcasted_iota(jnp.int32, new_scores.shape, 1)
    own_slot = lax.broadcasted_iota(jnp.int32, new_scores.shape, 0)
    new_ok = (new_slot >= start_col[...]) & (new_slot <= own_slot)
    cache_scores = jnp.where(cache_ok, cache_scores, -1e30)
    new_scores = jnp.where(new_ok, new_scores, -1e30)
    peak = jnp.maximum(
        jnp.max(cache_scores, axis=1, keepdims=True), jnp.max(new_scores, axis=1, keepdims=True)
    )
    cache_exp = jnp.exp(cache_scores - peak)
    new_exp = jnp.exp(new_scores - peak)
    total = jnp.sum(cache_exp, axis=1, keepdims=True) + jnp.sum(new_exp, axis=1, keepdims=True)
    cache_probs = (cache_exp / total).astype(jnp.bfloat16)
    new_probs = (new_exp / total).astype(jnp.bfloat16)
    mixed = jnp.dot(cache_probs, cache_values, preferred_element_type=jnp.float32) + jnp.dot(
        new_probs, vn_ref[...], preferred_element_type=jnp.float32
    )
    o_ref[...] = mixed.astype(o_ref.dtype)


def attend_kernel(queries, new_keys, new_values, pages, local_req, cached, positions):
    tokens, heads = queries.shape[0], queries.shape[1]
    page_count, page_len = pages.shape[0], pages.shape[2]
    span = page_count * page_len // cached.shape[0]
    own_cached = jnp.take(cached, local_req)
    lo_col = (local_req * span)[:, None]
    hi_col = lo_col + own_cached[:, None]
    start_col = (jnp.arange(tokens, dtype=jnp.int32) - positions + own_cached)[:, None]
    flat = lambda x: x.reshape(tokens, heads * HD)
    row_block = pl.BlockSpec((tokens, HD), lambda h: (0, h))
    page_block = lambda part: pl.BlockSpec((page_count, 1, page_len, HD), lambda h: (0, part, 0, h))
    whole = lambda x: pl.BlockSpec(x.shape, lambda h: (0,) * x.ndim)
    extras = (lo_col, hi_col, start_col)
    keys_seen = page_count * page_len + tokens
    out = pl.pallas_call(
        attention_kernel,
        grid=(heads,),
        in_specs=[row_block, page_block(0), page_block(1), row_block, row_block]
        + [whole(x) for x in extras],
        out_specs=row_block,
        out_shape=jax.ShapeDtypeStruct((tokens, heads * HD), jnp.bfloat16),
        cost_estimate=pl.CostEstimate(
            flops=4 * heads * tokens * keys_seen * HD,
            transcendentals=heads * tokens * keys_seen,
            bytes_accessed=2 * HD * heads * (2 * tokens + 2 * keys_seen),
        ),
    )(flat(queries), pages, pages, flat(new_keys), flat(new_values), *extras)
    return out


def share_pages(local_pool, groups):
    grouped = local_pool.reshape(
        local_pool.shape[0], 2, local_pool.shape[2], groups, local_pool.shape[3] // groups
    )
    shared = lax.all_to_all(grouped, "head", split_axis=3, concat_axis=0, tiled=True)
    return shared.reshape(shared.shape[0], 2, shared.shape[2], shared.shape[4])


def gather_by_all_to_all(block, axis):
    count = lax.axis_size(axis)
    copies = jnp.broadcast_to(block[None], (count,) + block.shape).reshape(
        (count * block.shape[0],) + block.shape[1:]
    )
    return lax.all_to_all(copies, axis, split_axis=0, concat_axis=0, tiled=True)


def shards(
    states,
    pre_gain,
    pre_shift,
    mlp_gain,
    mlp_shift,
    qkv_weight,
    qkv_bias,
    out_weight,
    out_bias,
    up_weight,
    up_bias,
    down_weight,
    down_bias,
    kv_cache,
    token_request,
    cached_len,
    page_table,
    migrations,
):
    gathered = lax.all_gather(states, "head", axis=1, tiled=True)
    qkv_full = gather_by_all_to_all(qkv_weight, "tok")
    out_full = lax.all_gather(out_weight, "tok", axis=1, tiled=True)
    wide = gathered.astype(jnp.float32)
    pre_normed = layer_norm(wide, pre_gain, pre_shift)
    mlp_normed = layer_norm(wide, mlp_gain, mlp_shift)
    tok_rows = gathered.shape[0]

    def feed(normed):
        hidden = jax.nn.gelu(
            jnp.dot(normed, up_weight, preferred_element_type=jnp.float32) + up_bias,
            approximate=False,
        ).astype(jnp.bfloat16)
        return jnp.dot(hidden, down_weight, preferred_element_type=jnp.float32).astype(jnp.bfloat16)

    feed_part = feed(mlp_normed)
    kv_cache, feed_part = lax.optimization_barrier((kv_cache, feed_part))
    page_pool = share_pages(kv_cache, lax.axis_size("head"))
    joined = jnp.dot(pre_normed, qkv_full, preferred_element_type=jnp.float32)
    joined = (joined + qkv_bias).reshape(tok_rows, -1, 3, HD)
    local_req = token_request - lax.axis_index("tok") * cached_len.shape[0]
    positions = token_positions(local_req, cached_len)
    queries = rotate(joined[:, :, 0], positions).astype(jnp.bfloat16)
    new_keys = rotate(joined[:, :, 1], positions).astype(jnp.bfloat16)
    new_values = joined[:, :, 2].astype(jnp.bfloat16)
    sources = migrations[:, 0]
    targets = migrations[:, 1]
    table = page_table.reshape(-1)
    match = table[:, None] == targets[None, :]
    moved_from = jnp.sum(jnp.where(match, sources[None, :], 0), axis=1)
    table = jnp.where(jnp.any(match, axis=1), moved_from, table)
    pages = page_pool[table]
    heads_out = attend_kernel(
        queries, new_keys, new_values, pages, local_req, cached_len, positions
    )
    attention_part = jnp.dot(heads_out, out_full, preferred_element_type=jnp.float32)
    bias_row = lax.dynamic_update_slice_in_dim(
        jnp.zeros((attention_part.shape[1],), jnp.float32),
        out_bias + down_bias,
        lax.axis_index("head") * out_bias.shape[0],
        axis=0,
    )
    both = (attention_part + feed_part + bias_row).astype(jnp.bfloat16)
    half = both.shape[0] // 2
    groups = lax.axis_size("head")
    later = lax.psum_scatter(both[half:], "head", scatter_dimension=1, tiled=True)
    spread = both[:half].reshape(half, groups, both.shape[1] // groups)
    swapped = lax.all_to_all(spread, "head", split_axis=1, concat_axis=1, tiled=True)
    first = jnp.sum(swapped.astype(jnp.float32), axis=1).astype(jnp.bfloat16)
    return jnp.concatenate([first, later], axis=0)


def solution(mesh):
    in_specs = (
        P("tok", "head"),
        P(),
        P(),
        P(),
        P(),
        P("tok", "head"),
        P("head"),
        P("head", "tok"),
        P("head"),
        P(None, "head"),
        P("head"),
        P("head", None),
        P("head"),
        P(("tok", "head"), None, None, None),
        P("tok"),
        P("tok"),
        P("tok", None),
        P("tok", None),
    )
    out_specs = P("tok", "head")
    return jax.shard_map(shards, mesh=mesh, in_specs=in_specs, out_specs=out_specs, check_vma=False)
```

```python
import jax
import jax.numpy as jnp
from jax import lax
from jax.sharding import PartitionSpec as P
from jax.experimental import pallas as pl
from jax.experimental.pallas import tpu as pltpu

HD = 128
ROT = 32


epsilon = 1e-05


def layer_norm(wide, gain, shift):
    row_mean = jnp.mean(wide, axis=1, keepdims=True)
    centred = wide - row_mean
    row_var = jnp.mean(centred * centred, axis=1, keepdims=True)
    return (centred * lax.rsqrt(row_var + epsilon) * gain + shift).astype(jnp.bfloat16)


def rotate(vectors, positions):
    half_rot = ROT // 2
    inv_freq = 10000.0 ** (-2.0 * jnp.arange(half_rot, dtype=jnp.float32) / ROT)
    angles = positions.astype(jnp.float32)[:, None] * inv_freq[None, :]
    cosine = jnp.cos(angles)[:, None, :]
    sine_part = jnp.sin(angles)[:, None, :]
    lower_half = vectors[..., :half_rot]
    upper_half = vectors[..., half_rot:ROT]
    return jnp.concatenate(
        [
            lower_half * cosine - upper_half * sine_part,
            upper_half * cosine + lower_half * sine_part,
            vectors[..., ROT:],
        ],
        axis=-1,
    )


def token_positions(local_req, cached):
    onehot = local_req[:, None] == jnp.arange(cached.shape[0], dtype=jnp.int32)[None, :]
    stretch_sizes = jnp.sum(onehot.astype(jnp.int32), axis=0)
    starts = jnp.cumsum(stretch_sizes) - stretch_sizes
    own_start = jnp.sum(jnp.where(onehot, starts[None, :], 0), axis=1)
    own_cached = jnp.sum(jnp.where(onehot, cached[None, :], 0), axis=1)
    return own_cached + jnp.arange(local_req.shape[0], dtype=jnp.int32) - own_start


def attend(queries, new_keys, new_values, cache_keys, cache_values, local_req, cached, positions):
    span = cache_keys.shape[0] // cached.shape[0]
    key_slot = jnp.arange(cache_keys.shape[0], dtype=jnp.int32)
    key_owner = key_slot // span
    key_place = key_slot % span
    cache_ok = (local_req[:, None] == key_owner[None, :]) & (
        key_place[None, :] < jnp.repeat(cached, span)[None, :]
    )
    new_ok = (local_req[:, None] == local_req[None, :]) & (positions[None, :] <= positions[:, None])
    allowed = jnp.concatenate([cache_ok, new_ok], axis=1)
    all_keys = jnp.concatenate([cache_keys, new_keys], axis=0)
    all_values = jnp.concatenate([cache_values, new_values], axis=0)
    scores = jnp.einsum(
        "thd,khd->htk", queries, all_keys, preferred_element_type=jnp.float32
    ) * HD ** (-0.5)
    scores = jnp.where(allowed[None], scores, -1e30)
    peak = jnp.max(scores, axis=2, keepdims=True)
    exp_scores = jnp.exp(scores - peak)
    attn_probs = (exp_scores / jnp.sum(exp_scores, axis=2, keepdims=True)).astype(jnp.bfloat16)
    return jnp.einsum(
        "htk,khd->thd", attn_probs, all_values, preferred_element_type=jnp.float32
    ).astype(jnp.bfloat16)


def attention_kernel(q_ref, kc_ref, vc_ref, kn_ref, vn_ref, lo_col, hi_col, start_col, o_ref):
    queries = q_ref[...]
    cache_keys = kc_ref[...].reshape(-1, queries.shape[1])
    cache_values = vc_ref[...].reshape(-1, queries.shape[1])
    dims = (((1,), (1,)), ((), ()))
    scale = HD ** (-0.5)
    cache_scores = lax.dot_general(queries, cache_keys, dims, preferred_element_type=jnp.float32) * scale
    new_scores = lax.dot_general(queries, kn_ref[...], dims, preferred_element_type=jnp.float32) * scale
    cache_slot = lax.broadcasted_iota(jnp.int32, cache_scores.shape, 1)
    cache_ok = (cache_slot >= lo_col[...]) & (cache_slot < hi_col[...])
    new_slot = lax.broadcasted_iota(jnp.int32, new_scores.shape, 1)
    own_slot = lax.broadcasted_iota(jnp.int32, new_scores.shape, 0) + pl.program_id(1) * queries.shape[0]
    new_ok = (new_slot >= start_col[...]) & (new_slot <= own_slot)
    cache_scores = jnp.where(cache_ok, cache_scores, -1e30)
    new_scores = jnp.where(new_ok, new_scores, -1e30)
    peak = jnp.maximum(
        jnp.max(cache_scores, axis=1, keepdims=True), jnp.max(new_scores, axis=1, keepdims=True)
    )
    cache_exp = jnp.exp(cache_scores - peak)
    new_exp = jnp.exp(new_scores - peak)
    total = jnp.sum(cache_exp, axis=1, keepdims=True) + jnp.sum(new_exp, axis=1, keepdims=True)
    cache_probs = (cache_exp / total).astype(jnp.bfloat16)
    new_probs = (new_exp / total).astype(jnp.bfloat16)
    mixed = jnp.dot(cache_probs, cache_values, preferred_element_type=jnp.float32) + jnp.dot(
        new_probs, vn_ref[...], preferred_element_type=jnp.float32
    )
    o_ref[...] = mixed.astype(o_ref.dtype)


def attend_kernel(queries, new_keys, new_values, pages, local_req, cached, positions):
    tokens, heads = queries.shape[0], queries.shape[1]
    page_count, page_len = pages.shape[0], pages.shape[2]
    span = page_count * page_len // cached.shape[0]
    own_cached = jnp.take(cached, local_req)
    lo_col = (local_req * span)[:, None]
    hi_col = lo_col + own_cached[:, None]
    start_col = (jnp.arange(tokens, dtype=jnp.int32) - positions + own_cached)[:, None]
    flat = lambda x: x.reshape(tokens, heads * HD)
    rows = tokens // 2
    tile_block = pl.BlockSpec((rows, HD), lambda h, i: (i, h))
    row_block = pl.BlockSpec((tokens, HD), lambda h, i: (0, h))
    page_block = lambda part: pl.BlockSpec((page_count, 1, page_len, HD), lambda h, i: (0, part, 0, h))
    column = lambda x: pl.BlockSpec((rows, 1), lambda h, i: (i, 0))
    extras = (lo_col, hi_col, start_col)
    keys_seen = page_count * page_len + tokens
    out = pl.pallas_call(
        attention_kernel,
        grid=(heads, 2),
        in_specs=[tile_block, page_block(0), page_block(1), row_block, row_block]
        + [column(x) for x in extras],
        out_specs=tile_block,
        out_shape=jax.ShapeDtypeStruct((tokens, heads * HD), jnp.bfloat16),
        cost_estimate=pl.CostEstimate(
            flops=4 * heads * tokens * keys_seen * HD,
            transcendentals=heads * tokens * keys_seen,
            bytes_accessed=2 * HD * heads * (2 * tokens + 2 * keys_seen),
        ),
    )(flat(queries), pages, pages, flat(new_keys), flat(new_values), *extras)
    return out


def share_pages(local_pool, groups):
    grouped = local_pool.reshape(
        local_pool.shape[0], 2, local_pool.shape[2], groups, local_pool.shape[3] // groups
    )
    shared = lax.all_to_all(grouped, "head", split_axis=3, concat_axis=0, tiled=True)
    return shared.reshape(shared.shape[0], 2, shared.shape[2], shared.shape[4])


def gather_by_all_to_all(block, axis):
    count = lax.axis_size(axis)
    copies = jnp.broadcast_to(block[None], (count,) + block.shape).reshape(
        (count * block.shape[0],) + block.shape[1:]
    )
    return lax.all_to_all(copies, axis, split_axis=0, concat_axis=0, tiled=True)


def shards(
    states,
    pre_gain,
    pre_shift,
    mlp_gain,
    mlp_shift,
    qkv_weight,
    qkv_bias,
    out_weight,
    out_bias,
    up_weight,
    up_bias,
    down_weight,
    down_bias,
    kv_cache,
    token_request,
    cached_len,
    page_table,
    migrations,
):
    gathered = lax.all_gather(states, "head", axis=1, tiled=True)
    qkv_full = gather_by_all_to_all(qkv_weight, "tok")
    out_full = lax.all_gather(out_weight, "tok", axis=1, tiled=True)
    wide = gathered.astype(jnp.float32)
    pre_normed = layer_norm(wide, pre_gain, pre_shift)
    mlp_normed = layer_norm(wide, mlp_gain, mlp_shift)
    tok_rows = gathered.shape[0]

    def feed(normed):
        hidden = jax.nn.gelu(
            jnp.dot(normed, up_weight, preferred_element_type=jnp.float32) + up_bias,
            approximate=False,
        ).astype(jnp.bfloat16)
        return jnp.dot(hidden, down_weight, preferred_element_type=jnp.float32).astype(jnp.bfloat16)

    feed_part = feed(mlp_normed)
    kv_cache, feed_part = lax.optimization_barrier((kv_cache, feed_part))
    page_pool = share_pages(kv_cache, lax.axis_size("head"))
    joined = jnp.dot(pre_normed, qkv_full, preferred_element_type=jnp.float32)
    joined = (joined + qkv_bias).reshape(tok_rows, -1, 3, HD)
    local_req = token_request - lax.axis_index("tok") * cached_len.shape[0]
    positions = token_positions(local_req, cached_len)
    queries = rotate(joined[:, :, 0], positions).astype(jnp.bfloat16)
    new_keys = rotate(joined[:, :, 1], positions).astype(jnp.bfloat16)
    new_values = joined[:, :, 2].astype(jnp.bfloat16)
    sources = migrations[:, 0]
    targets = migrations[:, 1]
    table = page_table.reshape(-1)
    match = table[:, None] == targets[None, :]
    moved_from = jnp.sum(jnp.where(match, sources[None, :], 0), axis=1)
    table = jnp.where(jnp.any(match, axis=1), moved_from, table)
    pages = page_pool[table]
    heads_out = attend_kernel(
        queries, new_keys, new_values, pages, local_req, cached_len, positions
    )
    attention_part = jnp.dot(heads_out, out_full, preferred_element_type=jnp.float32)
    bias_row = lax.dynamic_update_slice_in_dim(
        jnp.zeros((attention_part.shape[1],), jnp.float32),
        out_bias + down_bias,
        lax.axis_index("head") * out_bias.shape[0],
        axis=0,
    )
    return lax.psum_scatter(
        (attention_part + feed_part + bias_row).astype(jnp.bfloat16),
        "head",
        scatter_dimension=1,
        tiled=True,
    )


def solution(mesh):
    in_specs = (
        P("tok", "head"),
        P(),
        P(),
        P(),
        P(),
        P("tok", "head"),
        P("head"),
        P("head", "tok"),
        P("head"),
        P(None, "head"),
        P("head"),
        P("head", None),
        P("head"),
        P(("tok", "head"), None, None, None),
        P("tok"),
        P("tok"),
        P("tok", None),
        P("tok", None),
    )
    out_specs = P("tok", "head")
    return jax.shard_map(shards, mesh=mesh, in_specs=in_specs, out_specs=out_specs, check_vma=False)
```

```python
import jax
import jax.numpy as jnp
from jax import lax
from jax.sharding import PartitionSpec as P
from jax.experimental import pallas as pl
from jax.experimental.pallas import tpu as pltpu

HD = 128
ROT = 32


epsilon = 1e-05


def layer_norm(wide, gain, shift):
    row_mean = jnp.mean(wide, axis=1, keepdims=True)
    centred = wide - row_mean
    row_var = jnp.mean(centred * centred, axis=1, keepdims=True)
    return (centred * lax.rsqrt(row_var + epsilon) * gain + shift).astype(jnp.bfloat16)


def rotate(vectors, positions):
    half_rot = ROT // 2
    inv_freq = 10000.0 ** (-2.0 * jnp.arange(half_rot, dtype=jnp.float32) / ROT)
    angles = positions.astype(jnp.float32)[:, None] * inv_freq[None, :]
    cosine = jnp.cos(angles)[:, None, :]
    sine_part = jnp.sin(angles)[:, None, :]
    lower_half = vectors[..., :half_rot]
    upper_half = vectors[..., half_rot:ROT]
    return jnp.concatenate(
        [
            lower_half * cosine - upper_half * sine_part,
            upper_half * cosine + lower_half * sine_part,
            vectors[..., ROT:],
        ],
        axis=-1,
    )


def token_positions(local_req, cached):
    onehot = local_req[:, None] == jnp.arange(cached.shape[0], dtype=jnp.int32)[None, :]
    stretch_sizes = jnp.sum(onehot.astype(jnp.int32), axis=0)
    starts = jnp.cumsum(stretch_sizes) - stretch_sizes
    own_start = jnp.sum(jnp.where(onehot, starts[None, :], 0), axis=1)
    own_cached = jnp.sum(jnp.where(onehot, cached[None, :], 0), axis=1)
    return own_cached + jnp.arange(local_req.shape[0], dtype=jnp.int32) - own_start


def attend(queries, new_keys, new_values, cache_keys, cache_values, local_req, cached, positions):
    span = cache_keys.shape[0] // cached.shape[0]
    key_slot = jnp.arange(cache_keys.shape[0], dtype=jnp.int32)
    key_owner = key_slot // span
    key_place = key_slot % span
    cache_ok = (local_req[:, None] == key_owner[None, :]) & (
        key_place[None, :] < jnp.repeat(cached, span)[None, :]
    )
    new_ok = (local_req[:, None] == local_req[None, :]) & (positions[None, :] <= positions[:, None])
    allowed = jnp.concatenate([cache_ok, new_ok], axis=1)
    all_keys = jnp.concatenate([cache_keys, new_keys], axis=0)
    all_values = jnp.concatenate([cache_values, new_values], axis=0)
    scores = jnp.einsum(
        "thd,khd->htk", queries, all_keys, preferred_element_type=jnp.float32
    ) * HD ** (-0.5)
    scores = jnp.where(allowed[None], scores, -1e30)
    peak = jnp.max(scores, axis=2, keepdims=True)
    exp_scores = jnp.exp(scores - peak)
    attn_probs = (exp_scores / jnp.sum(exp_scores, axis=2, keepdims=True)).astype(jnp.bfloat16)
    return jnp.einsum(
        "htk,khd->thd", attn_probs, all_values, preferred_element_type=jnp.float32
    ).astype(jnp.bfloat16)


def attention_kernel(q_ref, kc_ref, vc_ref, kn_ref, vn_ref, lo_col, hi_col, start_col, o_ref):
    queries = q_ref[...]
    cache_keys = kc_ref[...].reshape(-1, queries.shape[1])
    cache_values = vc_ref[...].reshape(-1, queries.shape[1])
    dims = (((1,), (1,)), ((), ()))
    scale = HD ** (-0.5)
    cache_scores = lax.dot_general(queries, cache_keys, dims, preferred_element_type=jnp.float32) * scale
    new_scores = lax.dot_general(queries, kn_ref[...], dims, preferred_element_type=jnp.float32) * scale
    cache_slot = lax.broadcasted_iota(jnp.int32, cache_scores.shape, 1)
    cache_ok = (cache_slot >= lo_col[...]) & (cache_slot < hi_col[...])
    new_slot = lax.broadcasted_iota(jnp.int32, new_scores.shape, 1)
    own_slot = lax.broadcasted_iota(jnp.int32, new_scores.shape, 0) + pl.program_id(1) * queries.shape[0]
    new_ok = (new_slot >= start_col[...]) & (new_slot <= own_slot)
    cache_scores = jnp.where(cache_ok, cache_scores, -1e30)
    new_scores = jnp.where(new_ok, new_scores, -1e30)
    peak = jnp.maximum(
        jnp.max(cache_scores, axis=1, keepdims=True), jnp.max(new_scores, axis=1, keepdims=True)
    )
    cache_exp = jnp.exp(cache_scores - peak)
    new_exp = jnp.exp(new_scores - peak)
    total = jnp.sum(cache_exp, axis=1, keepdims=True) + jnp.sum(new_exp, axis=1, keepdims=True)
    cache_probs = (cache_exp / total).astype(jnp.bfloat16)
    new_probs = (new_exp / total).astype(jnp.bfloat16)
    mixed = jnp.dot(cache_probs, cache_values, preferred_element_type=jnp.float32) + jnp.dot(
        new_probs, vn_ref[...], preferred_element_type=jnp.float32
    )
    o_ref[...] = mixed.astype(o_ref.dtype)


def attend_kernel(queries, new_keys, new_values, pages, local_req, cached, positions):
    tokens, heads = queries.shape[0], queries.shape[1]
    page_count, page_len = pages.shape[0], pages.shape[2]
    span = page_count * page_len // cached.shape[0]
    own_cached = jnp.take(cached, local_req)
    lo_col = (local_req * span)[:, None]
    hi_col = lo_col + own_cached[:, None]
    start_col = (jnp.arange(tokens, dtype=jnp.int32) - positions + own_cached)[:, None]
    flat = lambda x: x.reshape(tokens, heads * HD)
    rows = tokens // 2
    tile_block = pl.BlockSpec((rows, HD), lambda h, i: (i, h))
    row_block = pl.BlockSpec((tokens, HD), lambda h, i: (0, h))
    page_block = lambda part: pl.BlockSpec((page_count, 1, page_len, HD), lambda h, i: (0, part, 0, h))
    column = lambda x: pl.BlockSpec((rows, 1), lambda h, i: (i, 0))
    extras = (lo_col, hi_col, start_col)
    keys_seen = page_count * page_len + tokens
    out = pl.pallas_call(
        attention_kernel,
        grid=(heads, 2),
        in_specs=[tile_block, page_block(0), page_block(1), row_block, row_block]
        + [column(x) for x in extras],
        out_specs=tile_block,
        out_shape=jax.ShapeDtypeStruct((tokens, heads * HD), jnp.bfloat16),
        cost_estimate=pl.CostEstimate(
            flops=4 * heads * tokens * keys_seen * HD,
            transcendentals=heads * tokens * keys_seen,
            bytes_accessed=2 * HD * heads * (2 * tokens + 2 * keys_seen),
        ),
    )(flat(queries), pages, pages, flat(new_keys), flat(new_values), *extras)
    return out


def share_pages(local_pool, groups):
    grouped = local_pool.reshape(
        local_pool.shape[0], 2, local_pool.shape[2], groups, local_pool.shape[3] // groups
    )
    shared = lax.all_to_all(grouped, "head", split_axis=3, concat_axis=0, tiled=True)
    return shared.reshape(shared.shape[0], 2, shared.shape[2], shared.shape[4])


def gather_by_all_to_all(block, axis):
    count = lax.axis_size(axis)
    copies = jnp.broadcast_to(block[None], (count,) + block.shape).reshape(
        (count * block.shape[0],) + block.shape[1:]
    )
    return lax.all_to_all(copies, axis, split_axis=0, concat_axis=0, tiled=True)


def shards(
    states,
    pre_gain,
    pre_shift,
    mlp_gain,
    mlp_shift,
    qkv_weight,
    qkv_bias,
    out_weight,
    out_bias,
    up_weight,
    up_bias,
    down_weight,
    down_bias,
    kv_cache,
    token_request,
    cached_len,
    page_table,
    migrations,
):
    gathered = lax.all_gather(states, "head", axis=1, tiled=True)
    page_pool = share_pages(kv_cache, lax.axis_size("head"))
    qkv_weight, page_pool = lax.optimization_barrier((qkv_weight, page_pool))
    qkv_full = gather_by_all_to_all(qkv_weight, "tok")
    out_full = lax.all_gather(out_weight, "tok", axis=1, tiled=True)
    wide = gathered.astype(jnp.float32)
    pre_normed = layer_norm(wide, pre_gain, pre_shift)
    mlp_normed = layer_norm(wide, mlp_gain, mlp_shift)
    tok_rows = gathered.shape[0]

    def feed(normed):
        hidden = jax.nn.gelu(
            jnp.dot(normed, up_weight, preferred_element_type=jnp.float32) + up_bias,
            approximate=False,
        ).astype(jnp.bfloat16)
        return jnp.dot(hidden, down_weight, preferred_element_type=jnp.float32).astype(jnp.bfloat16)

    feed_part = feed(mlp_normed)
    qkv_full, feed_part = lax.optimization_barrier((qkv_full, feed_part))
    joined = jnp.dot(pre_normed, qkv_full, preferred_element_type=jnp.float32)
    joined = (joined + qkv_bias).reshape(tok_rows, -1, 3, HD)
    local_req = token_request - lax.axis_index("tok") * cached_len.shape[0]
    positions = token_positions(local_req, cached_len)
    queries = rotate(joined[:, :, 0], positions).astype(jnp.bfloat16)
    new_keys = rotate(joined[:, :, 1], positions).astype(jnp.bfloat16)
    new_values = joined[:, :, 2].astype(jnp.bfloat16)
    sources = migrations[:, 0]
    targets = migrations[:, 1]
    table = page_table.reshape(-1)
    match = table[:, None] == targets[None, :]
    moved_from = jnp.sum(jnp.where(match, sources[None, :], 0), axis=1)
    table = jnp.where(jnp.any(match, axis=1), moved_from, table)
    pages = page_pool[table]
    heads_out = attend_kernel(
        queries, new_keys, new_values, pages, local_req, cached_len, positions
    )
    attention_part = jnp.dot(heads_out, out_full, preferred_element_type=jnp.float32)
    bias_row = lax.dynamic_update_slice_in_dim(
        jnp.zeros((attention_part.shape[1],), jnp.float32),
        out_bias + down_bias,
        lax.axis_index("head") * out_bias.shape[0],
        axis=0,
    )
    return lax.psum_scatter(
        (attention_part + feed_part + bias_row).astype(jnp.bfloat16),
        "head",
        scatter_dimension=1,
        tiled=True,
    )


def solution(mesh):
    in_specs = (
        P("tok", "head"),
        P(),
        P(),
        P(),
        P(),
        P("tok", "head"),
        P("head"),
        P("head", "tok"),
        P("head"),
        P(None, "head"),
        P("head"),
        P("head", None),
        P("head"),
        P(("tok", "head"), None, None, None),
        P("tok"),
        P("tok"),
        P("tok", None),
        P("tok", None),
    )
    out_specs = P("tok", "head")
    return jax.shard_map(shards, mesh=mesh, in_specs=in_specs, out_specs=out_specs, check_vma=False)
```

```python
import jax
import jax.numpy as jnp
from jax import lax
from jax.sharding import PartitionSpec as P
from jax.experimental import pallas as pl
from jax.experimental.pallas import tpu as pltpu

HD = 128
ROT = 32


epsilon = 1e-05


def layer_norm(wide, gain, shift):
    row_mean = jnp.mean(wide, axis=1, keepdims=True)
    centred = wide - row_mean
    row_var = jnp.mean(centred * centred, axis=1, keepdims=True)
    return (centred * lax.rsqrt(row_var + epsilon) * gain + shift).astype(jnp.bfloat16)


def rotate(vectors, positions):
    half_rot = ROT // 2
    inv_freq = 10000.0 ** (-2.0 * jnp.arange(half_rot, dtype=jnp.float32) / ROT)
    angles = positions.astype(jnp.float32)[:, None] * inv_freq[None, :]
    cosine = jnp.cos(angles)[:, None, :]
    sine_part = jnp.sin(angles)[:, None, :]
    lower_half = vectors[..., :half_rot]
    upper_half = vectors[..., half_rot:ROT]
    return jnp.concatenate(
        [
            lower_half * cosine - upper_half * sine_part,
            upper_half * cosine + lower_half * sine_part,
            vectors[..., ROT:],
        ],
        axis=-1,
    )


def token_positions(local_req, cached):
    onehot = local_req[:, None] == jnp.arange(cached.shape[0], dtype=jnp.int32)[None, :]
    stretch_sizes = jnp.sum(onehot.astype(jnp.int32), axis=0)
    starts = jnp.cumsum(stretch_sizes) - stretch_sizes
    own_start = jnp.sum(jnp.where(onehot, starts[None, :], 0), axis=1)
    own_cached = jnp.sum(jnp.where(onehot, cached[None, :], 0), axis=1)
    return own_cached + jnp.arange(local_req.shape[0], dtype=jnp.int32) - own_start


def attend(queries, new_keys, new_values, cache_keys, cache_values, local_req, cached, positions):
    span = cache_keys.shape[0] // cached.shape[0]
    key_slot = jnp.arange(cache_keys.shape[0], dtype=jnp.int32)
    key_owner = key_slot // span
    key_place = key_slot % span
    cache_ok = (local_req[:, None] == key_owner[None, :]) & (
        key_place[None, :] < jnp.repeat(cached, span)[None, :]
    )
    new_ok = (local_req[:, None] == local_req[None, :]) & (positions[None, :] <= positions[:, None])
    allowed = jnp.concatenate([cache_ok, new_ok], axis=1)
    all_keys = jnp.concatenate([cache_keys, new_keys], axis=0)
    all_values = jnp.concatenate([cache_values, new_values], axis=0)
    scores = jnp.einsum(
        "thd,khd->htk", queries, all_keys, preferred_element_type=jnp.float32
    ) * HD ** (-0.5)
    scores = jnp.where(allowed[None], scores, -1e30)
    peak = jnp.max(scores, axis=2, keepdims=True)
    exp_scores = jnp.exp(scores - peak)
    attn_probs = (exp_scores / jnp.sum(exp_scores, axis=2, keepdims=True)).astype(jnp.bfloat16)
    return jnp.einsum(
        "htk,khd->thd", attn_probs, all_values, preferred_element_type=jnp.float32
    ).astype(jnp.bfloat16)


def attention_kernel(q_ref, kc_ref, vc_ref, kn_ref, vn_ref, lo_col, hi_col, start_col, o_ref):
    queries = q_ref[...]
    cache_keys = kc_ref[...].reshape(-1, queries.shape[1])
    cache_values = vc_ref[...].reshape(-1, queries.shape[1])
    dims = (((1,), (1,)), ((), ()))
    scale = HD ** (-0.5)
    cache_scores = lax.dot_general(queries, cache_keys, dims, preferred_element_type=jnp.float32) * scale
    new_scores = lax.dot_general(queries, kn_ref[...], dims, preferred_element_type=jnp.float32) * scale
    cache_slot = lax.broadcasted_iota(jnp.int32, cache_scores.shape, 1)
    cache_ok = (cache_slot >= lo_col[...]) & (cache_slot < hi_col[...])
    new_slot = lax.broadcasted_iota(jnp.int32, new_scores.shape, 1)
    own_slot = lax.broadcasted_iota(jnp.int32, new_scores.shape, 0) + pl.program_id(1) * queries.shape[0]
    new_ok = (new_slot >= start_col[...]) & (new_slot <= own_slot)
    cache_scores = jnp.where(cache_ok, cache_scores, -1e30)
    new_scores = jnp.where(new_ok, new_scores, -1e30)
    peak = jnp.maximum(
        jnp.max(cache_scores, axis=1, keepdims=True), jnp.max(new_scores, axis=1, keepdims=True)
    )
    cache_exp = jnp.exp(cache_scores - peak)
    new_exp = jnp.exp(new_scores - peak)
    total = jnp.sum(cache_exp, axis=1, keepdims=True) + jnp.sum(new_exp, axis=1, keepdims=True)
    cache_probs = (cache_exp / total).astype(jnp.bfloat16)
    new_probs = (new_exp / total).astype(jnp.bfloat16)
    mixed = jnp.dot(cache_probs, cache_values, preferred_element_type=jnp.float32) + jnp.dot(
        new_probs, vn_ref[...], preferred_element_type=jnp.float32
    )
    o_ref[...] = mixed.astype(o_ref.dtype)


def attend_kernel(queries, new_keys, new_values, pages, local_req, cached, positions):
    tokens, heads = queries.shape[0], queries.shape[1]
    page_count, page_len = pages.shape[0], pages.shape[2]
    span = page_count * page_len // cached.shape[0]
    own_cached = jnp.take(cached, local_req)
    lo_col = (local_req * span)[:, None]
    hi_col = lo_col + own_cached[:, None]
    start_col = (jnp.arange(tokens, dtype=jnp.int32) - positions + own_cached)[:, None]
    flat = lambda x: x.reshape(tokens, heads * HD)
    rows = tokens // 4
    tile_block = pl.BlockSpec((rows, HD), lambda h, i: (i, h))
    row_block = pl.BlockSpec((tokens, HD), lambda h, i: (0, h))
    page_block = lambda part: pl.BlockSpec((page_count, 1, page_len, HD), lambda h, i: (0, part, 0, h))
    column = lambda x: pl.BlockSpec((rows, 1), lambda h, i: (i, 0))
    extras = (lo_col, hi_col, start_col)
    keys_seen = page_count * page_len + tokens
    out = pl.pallas_call(
        attention_kernel,
        grid=(heads, 4),
        in_specs=[tile_block, page_block(0), page_block(1), row_block, row_block]
        + [column(x) for x in extras],
        out_specs=tile_block,
        out_shape=jax.ShapeDtypeStruct((tokens, heads * HD), jnp.bfloat16),
        cost_estimate=pl.CostEstimate(
            flops=4 * heads * tokens * keys_seen * HD,
            transcendentals=heads * tokens * keys_seen,
            bytes_accessed=2 * HD * heads * (2 * tokens + 2 * keys_seen),
        ),
    )(flat(queries), pages, pages, flat(new_keys), flat(new_values), *extras)
    return out


def share_pages(local_pool, groups):
    grouped = local_pool.reshape(
        local_pool.shape[0], 2, local_pool.shape[2], groups, local_pool.shape[3] // groups
    )
    shared = lax.all_to_all(grouped, "head", split_axis=3, concat_axis=0, tiled=True)
    return shared.reshape(shared.shape[0], 2, shared.shape[2], shared.shape[4])


def gather_by_all_to_all(block, axis):
    count = lax.axis_size(axis)
    copies = jnp.broadcast_to(block[None], (count,) + block.shape).reshape(
        (count * block.shape[0],) + block.shape[1:]
    )
    return lax.all_to_all(copies, axis, split_axis=0, concat_axis=0, tiled=True)


def shards(
    states,
    pre_gain,
    pre_shift,
    mlp_gain,
    mlp_shift,
    qkv_weight,
    qkv_bias,
    out_weight,
    out_bias,
    up_weight,
    up_bias,
    down_weight,
    down_bias,
    kv_cache,
    token_request,
    cached_len,
    page_table,
    migrations,
):
    gathered = lax.all_gather(states, "head", axis=1, tiled=True)
    qkv_full = gather_by_all_to_all(qkv_weight, "tok")
    out_full = lax.all_gather(out_weight, "tok", axis=1, tiled=True)
    wide = gathered.astype(jnp.float32)
    pre_normed = layer_norm(wide, pre_gain, pre_shift)
    mlp_normed = layer_norm(wide, mlp_gain, mlp_shift)
    tok_rows = gathered.shape[0]

    def feed(normed):
        hidden = jax.nn.gelu(
            jnp.dot(normed, up_weight, preferred_element_type=jnp.float32) + up_bias,
            approximate=False,
        ).astype(jnp.bfloat16)
        return jnp.dot(hidden, down_weight, preferred_element_type=jnp.float32).astype(jnp.bfloat16)

    feed_part = feed(mlp_normed)
    kv_cache, feed_part = lax.optimization_barrier((kv_cache, feed_part))
    page_pool = share_pages(kv_cache, lax.axis_size("head"))
    joined = jnp.dot(pre_normed, qkv_full, preferred_element_type=jnp.float32)
    joined = (joined + qkv_bias).reshape(tok_rows, -1, 3, HD)
    local_req = token_request - lax.axis_index("tok") * cached_len.shape[0]
    positions = token_positions(local_req, cached_len)
    queries = rotate(joined[:, :, 0], positions).astype(jnp.bfloat16)
    new_keys = rotate(joined[:, :, 1], positions).astype(jnp.bfloat16)
    new_values = joined[:, :, 2].astype(jnp.bfloat16)
    sources = migrations[:, 0]
    targets = migrations[:, 1]
    table = page_table.reshape(-1)
    match = table[:, None] == targets[None, :]
    moved_from = jnp.sum(jnp.where(match, sources[None, :], 0), axis=1)
    table = jnp.where(jnp.any(match, axis=1), moved_from, table)
    pages = page_pool[table]
    heads_out = attend_kernel(
        queries, new_keys, new_values, pages, local_req, cached_len, positions
    )
    attention_part = jnp.dot(heads_out, out_full, preferred_element_type=jnp.float32)
    bias_row = lax.dynamic_update_slice_in_dim(
        jnp.zeros((attention_part.shape[1],), jnp.float32),
        out_bias + down_bias,
        lax.axis_index("head") * out_bias.shape[0],
        axis=0,
    )
    return lax.psum_scatter(
        (attention_part + feed_part + bias_row).astype(jnp.bfloat16),
        "head",
        scatter_dimension=1,
        tiled=True,
    )


def solution(mesh):
    in_specs = (
        P("tok", "head"),
        P(),
        P(),
        P(),
        P(),
        P("tok", "head"),
        P("head"),
        P("head", "tok"),
        P("head"),
        P(None, "head"),
        P("head"),
        P("head", None),
        P("head"),
        P(("tok", "head"), None, None, None),
        P("tok"),
        P("tok"),
        P("tok", None),
        P("tok", None),
    )
    out_specs = P("tok", "head")
    return jax.shard_map(shards, mesh=mesh, in_specs=in_specs, out_specs=out_specs, check_vma=False)
```
